512 devices in a mesh: seq: 64 (over y, x, core), fsdp: 8 (over z).
Axes of the slice: x: 4, y: 8, z: 8, core: 2. Of those that a mesh axis runs over, the one named last changes fastest.
Arguments:
- queries: bfloat16 [32768, 2048], P('seq', 'fsdp'), may hold values from -6 to 6
- keys: bfloat16 [32768, 2048], P('seq', 'fsdp'), may hold values from -6 to 6
- values: bfloat16 [32768, 2048], P('seq', 'fsdp'), may hold values from -6 to 6
- feature_weight: bfloat16 [16, 128, 128], P(None, 'fsdp', 'seq'), may hold values from -0.5 to 0.5
- norm_gain: bfloat16 [16, 128], P('fsdp'), may hold values from 0.099609375 to 1.8984375
- doc_bounds: int32 [4, 2], replicated, may hold values from 0 to 256, as said below
- out_grad: bfloat16 [32768, 2048], P('seq', 'fsdp'), may hold values from -6 to 6
Outputs:
- mixed: bfloat16 [32768, 2048], P('seq', 'fsdp')
- query_grad: bfloat16 [32768, 2048], P('seq', 'fsdp')
- key_grad: bfloat16 [32768, 2048], P('seq', 'fsdp')
- value_grad: bfloat16 [32768, 2048], P('seq', 'fsdp')
- weight_grad: float32 [16, 128, 128], P(None, 'fsdp', 'seq')
- gain_grad: float32 [16, 128], P('fsdp')
The draws below stay inside these ranges and needn't reach their ends.
Inputs may be any that keep to these rules, and one draw needn't show every extreme that they name: `doc_bounds`: the rows list the 4 documents in order: column 0 is the first block and column 1 the block after the last; the first document starts at block 0, each ends where the next starts, the last ends at block 256; every document holds one block or more of 128 tokens.
All inputs are finite; a program needn't handle non-finite values.
Results may differ from the reference program's by a relative error of at most 0.015.
Values may be sent and summed in bfloat16 or wider, within the bound.
No kernel may reach another device: no remote copies, remote signals or barrier semaphores. Data moves between devices by JAX's collectives and lax.ppermute only.
A program may use at most 64 MiB of HBM per device.

```python
from functools import partial
import jax
import jax.numpy as jnp
from jax import lax

H = 16
HS = 128
BLK = 128
DOCS = 4
HD = 2048
LEN = 32768
NBLK = 256


def draw_doc_bounds(key, part):
    borders = jax.random.permutation(key, NBLK - 1)[:DOCS - 1] + 1
    borders = jnp.sort(borders).astype(jnp.int32)
    starts = jnp.concatenate([jnp.zeros((1,), jnp.int32), borders])
    finishes = jnp.concatenate([borders, jnp.full((1,), NBLK, jnp.int32)])
    return jnp.stack([starts, finishes], axis=1)


def shard_levels(rng, shape, shards, least, high):
    gain = 1.0
    for axis_at, parts in shards:
        steps = jax.random.uniform(jax.random.fold_in(jax.random.fold_in(rng, 6), axis_at), (parts,), jnp.float32, least / len(shards), high / len(shards))
        gain = gain * jnp.repeat(jnp.exp(steps), shape[axis_at] // parts).reshape((-1,) + (1,) * (len(shape) - 1 - axis_at))
    return gain


def gaussian(rng, shape, deviation, bound, shards=(), held_as=jnp.bfloat16):
    values = jax.random.normal(rng, shape, jnp.float32) * deviation
    if len(shards) > 0:
        values = shard_levels(rng, shape, shards, -0.22, 0.18) * values
    return jnp.clip(values, min=-bound, max=bound).astype(held_as)


def setup_inputs(seed: int = 0) -> dict:
    seeds = jax.random.split(jax.random.key(seed), 8)
    queries = gaussian(seeds[0], (LEN, HD), 1.0, 6.0, ((0, 64), (1, 8)))
    keys = gaussian(seeds[1], (LEN, HD), 1.0, 6.0, ((0, 64), (1, 8)))
    values = gaussian(seeds[2], (LEN, HD), 1.0, 6.0, ((0, 64), (1, 8)))
    feature_weight = gaussian(seeds[3], (H, HS, HS), HS ** -0.5, 0.5, ((1, 8), (2, 64)))
    norm_gain = jnp.clip(1.0 + 0.18 * jax.random.normal(seeds[4], (H, HS), jnp.float32), 0.099609375, 1.8984375).astype(jnp.bfloat16)
    doc_bounds = draw_doc_bounds(jax.random.fold_in(seeds[7], 71), 0)
    out_grad = gaussian(seeds[6], (LEN, HD), 1.0, 6.0, ((0, 64), (1, 8)))
    return dict(queries=queries, keys=keys, values=values, feature_weight=feature_weight, norm_gain=norm_gain, doc_bounds=doc_bounds, out_grad=out_grad)


epsilon = 1.0

def rounded(array):
    return lax.optimization_barrier(array.astype(jnp.bfloat16)).astype(jnp.float32)

def one_head(starts_here, items):
    query_rows, key_rows, value_rows, grad_rows, weight_f, gain_f = items
    block_shape = (NBLK, BLK, HS)
    query_blocks = query_rows.reshape(block_shape).astype(jnp.float32)
    key_blocks = key_rows.reshape(block_shape).astype(jnp.float32)
    value_blocks = value_rows.reshape(block_shape).astype(jnp.float32)
    grad_y = grad_rows.reshape(block_shape).astype(jnp.float32)
    qfeat = rounded(jnp.einsum('btd,de->bte', query_blocks, weight_f))
    kfeat = rounded(jnp.einsum('btd,de->bte', key_blocks, weight_f))
    updates = jnp.einsum('bte,btf->bef', kfeat, value_blocks)
    zero_state = jnp.zeros((HS, HS), jnp.float32)

    def forward_step(running, item):
        update, opened = item
        held = jnp.where(opened, zero_state, running)
        return (held + update, held)
    _, states = lax.scan(forward_step, zero_state, (updates, starts_here))
    state_half = rounded(states)
    causal = jnp.arange(BLK)[:, None] >= jnp.arange(BLK)[None, :]
    scores = jnp.einsum('bte,bse->bts', qfeat, kfeat)
    prob_half = rounded(jnp.where(causal, scores, 0.0))
    mixed_f = jnp.einsum('bte,bef->btf', qfeat, state_half) + jnp.einsum('bts,bsf->btf', prob_half, value_blocks)
    inverse = lax.rsqrt(lax.optimization_barrier(jnp.mean(mixed_f * mixed_f, axis=-1, keepdims=True)) + epsilon)
    mixed = (mixed_f * inverse * gain_f).astype(jnp.bfloat16)
    scaled = grad_y * gain_f
    grad_mix = inverse * (scaled - mixed_f * inverse * inverse * lax.optimization_barrier(jnp.mean(scaled * mixed_f, axis=-1, keepdims=True)))
    grad_half = rounded(grad_mix)
    gain_part = lax.optimization_barrier(jnp.sum(grad_y * mixed_f * inverse, axis=(0, 1)))
    state_grads = jnp.einsum('bte,btf->bef', qfeat, grad_half)

    def backward_step(running, item):
        grad_term, opened = item
        return (jnp.where(opened, zero_state, running + grad_term), running)
    _, suffix = lax.scan(backward_step, zero_state, (state_grads, starts_here), reverse=True)
    suffix_half = rounded(suffix)
    dot_grads = rounded(jnp.where(causal, jnp.einsum('btf,bsf->bts', grad_half, value_blocks), 0.0))
    qfeat_grad = rounded(jnp.einsum('btf,bef->bte', grad_half, state_half) + jnp.einsum('bts,bse->bte', dot_grads, kfeat))
    kfeat_grad = rounded(jnp.einsum('bsf,bef->bse', value_blocks, suffix_half) + jnp.einsum('bts,bte->bse', dot_grads, qfeat))
    value_grad = (jnp.einsum('bse,bef->bsf', kfeat, suffix_half) + jnp.einsum('bts,btf->bsf', prob_half, grad_half)).astype(jnp.bfloat16)
    query_grad = jnp.einsum('bte,de->btd', qfeat_grad, weight_f).astype(jnp.bfloat16)
    key_grad = jnp.einsum('bte,de->btd', kfeat_grad, weight_f).astype(jnp.bfloat16)
    weight_part = jnp.einsum('btd,bte->de', query_blocks, qfeat_grad) + jnp.einsum('btd,bte->de', key_blocks, kfeat_grad)
    flat_shape = (LEN, HS)
    return (mixed.reshape(flat_shape), query_grad.reshape(flat_shape), key_grad.reshape(flat_shape), value_grad.reshape(flat_shape), weight_part, gain_part)

def to_heads(rows):
    return rows.reshape(LEN, H, HS).transpose(1, 0, 2)

def from_heads(stacked):
    return stacked.transpose(1, 0, 2).reshape(LEN, H * HS)

def reference(queries, keys, values, feature_weight, norm_gain, doc_bounds, out_grad):
    block_ids = jnp.arange(NBLK, dtype=jnp.int32)
    starts_here = jnp.any(doc_bounds[:, 0].astype(jnp.int32)[None, :] == block_ids[:, None], axis=1)
    items = (to_heads(queries), to_heads(keys), to_heads(values), to_heads(out_grad), feature_weight.astype(jnp.float32), norm_gain.astype(jnp.float32))
    results = lax.map(partial(one_head, starts_here), items)
    mixed, query_grad, key_grad, value_grad, weight_parts, gain_parts = results
    factor = LEN ** (-0.5)
    return (from_heads(mixed), from_heads(query_grad), from_heads(key_grad), from_heads(value_grad), weight_parts * factor, gain_parts * factor)
```

```python
import jax
import jax.numpy as jnp
from jax import lax
from jax.sharding import PartitionSpec as P

HS = 128
BLK = 128


epsilon = 1.0
HIGH = lax.Precision.HIGHEST


def shifted(x, dist, backward):
    count = lax.axis_size("seq")
    if backward:
        pairs = [(i, i - dist) for i in range(dist, count)]
    else:
        pairs = [(i, i + dist) for i in range(count - dist)]
    return lax.ppermute(x, "seq", pairs)


def carried_in(aggregate, opens, backward):
    count = lax.axis_size("seq")
    place = lax.axis_index("seq")
    sign = 1 if backward else -1
    near = shifted(aggregate, 1, backward)
    far = shifted(aggregate, 2, backward)
    one = place + sign
    state = jnp.where(opens(one, one), near, far + near)
    covered = 2
    while covered < count:
        far = shifted(state, covered, backward)
        lo, hi = (place + 1, place + covered) if backward else (place - covered, place - 1)
        state = jnp.where(opens(lo, hi), state, far + state)
        covered *= 2
    return state


def project(rows, weight):
    return jnp.einsum("bthd,hde->bthe", rows, weight, preferred_element_type=jnp.float32).astype(
        jnp.bfloat16
    )


def local(queries, keys, values, feature_weight, norm_gain, doc_bounds, out_grad):
    head_groups = lax.all_to_all(feature_weight, "fsdp", split_axis=0, concat_axis=1, tiled=True)
    weight_local = lax.all_gather(head_groups, "seq", axis=2, tiled=True)
    head_count = weight_local.shape[0]
    tokens_here = queries.shape[0]
    block_count = tokens_here // BLK
    block_shape = (block_count, BLK, head_count, HS)
    query_blocks = queries.reshape(block_shape)
    key_blocks = keys.reshape(block_shape)
    value_blocks = values.reshape(block_shape)

    place = lax.axis_index("seq")
    starts = doc_bounds[:, 0]
    start_device = starts // block_count

    def opens(lo, hi):
        return jnp.any((start_device >= lo) & (start_device <= hi))

    block_ids = place * block_count + jnp.arange(block_count, dtype=jnp.int32)
    starts_here = jnp.any(starts[None, :] == block_ids[:, None], axis=1)
    opened = jnp.cumsum(starts_here.astype(jnp.int32))
    reach_left = opened == 0
    reach_right = opened[-1] - opened == 0

    raw_updates = jnp.einsum(
        "bthd,bthf->bhdf", key_blocks, value_blocks, preferred_element_type=jnp.float32
    )
    zero_state = jnp.zeros(raw_updates.shape[1:], jnp.float32)
    running = zero_state
    prefix_list = []
    for position in range(block_count):
        held = jnp.where(starts_here[position], zero_state, running)
        prefix_list.append(held)
        running = held + raw_updates[position]
    entering = carried_in(running, opens, False)
    raw_states = jnp.stack(prefix_list) + jnp.where(
        reach_left[:, None, None, None], entering[None], 0.0
    )

    qfeat = project(query_blocks, weight_local)
    kfeat = project(key_blocks, weight_local)
    weight_f = weight_local.astype(jnp.float32)
    states = jnp.einsum("hde,bhdf->bhef", weight_f, raw_states, precision=HIGH)
    state_half = states.astype(jnp.bfloat16)
    causal = jnp.arange(BLK)[:, None] >= jnp.arange(BLK)[None, :]
    scores = jnp.einsum("bthe,bshe->bhts", qfeat, kfeat, preferred_element_type=jnp.float32)
    prob_half = jnp.where(causal, scores, 0.0).astype(jnp.bfloat16)
    mixed_f = jnp.einsum("bthe,bhef->bthf", qfeat, state_half, preferred_element_type=jnp.float32)
    mixed_f = mixed_f + jnp.einsum(
        "bhts,bshf->bthf", prob_half, value_blocks, preferred_element_type=jnp.float32
    )
    gains = norm_gain.astype(jnp.float32)
    inverse = lax.rsqrt(jnp.mean(mixed_f * mixed_f, axis=-1, keepdims=True) + epsilon)
    mixed = (mixed_f * inverse * gains).astype(jnp.bfloat16)
    grad_y = out_grad.reshape(block_shape).astype(jnp.float32)
    scaled = grad_y * gains
    grad_mix = inverse * (
        scaled - mixed_f * inverse * inverse * jnp.mean(scaled * mixed_f, axis=-1, keepdims=True)
    )
    grad_half = grad_mix.astype(jnp.bfloat16)
    gain_part = jnp.sum(grad_y * mixed_f * inverse, axis=(0, 1))
    gain_sum = lax.psum(gain_part, "seq")

    state_grads = jnp.einsum(
        "bthe,bthf->bhef", qfeat, grad_half, preferred_element_type=jnp.float32
    )
    dot_grads = jnp.einsum(
        "bthf,bshf->bhts", grad_half, value_blocks, preferred_element_type=jnp.float32
    )
    dot_half = jnp.where(causal, dot_grads, 0.0).astype(jnp.bfloat16)
    qfeat_grad = jnp.einsum(
        "bthf,bhef->bthe", grad_half, state_half, preferred_element_type=jnp.float32
    )
    qfeat_grad = (
        qfeat_grad
        + jnp.einsum("bhts,bshe->bthe", dot_half, kfeat, preferred_element_type=jnp.float32)
    ).astype(jnp.bfloat16)
    kfeat_inner = jnp.einsum(
        "bhts,bthe->bshe", dot_half, qfeat, preferred_element_type=jnp.float32
    )
    weight_part = jnp.einsum(
        "bthd,bthe->hde", query_blocks, qfeat_grad, preferred_element_type=jnp.float32
    )
    weight_part = weight_part + jnp.einsum(
        "bthd,bthe->hde", key_blocks, kfeat_inner.astype(jnp.bfloat16),
        preferred_element_type=jnp.float32,
    )
    weight_part = weight_part + jnp.einsum(
        "bhdf,bhef->hde", raw_states, state_grads, precision=HIGH
    )
    weight_columns = lax.psum_scatter(weight_part, "seq", scatter_dimension=2, tiled=True)
    owned_grad = lax.all_to_all(weight_columns, "fsdp", split_axis=1, concat_axis=0, tiled=True)

    running = zero_state
    suffix_list = [zero_state] * block_count
    for position in reversed(range(block_count)):
        suffix_list[position] = running
        running = jnp.where(starts_here[position], zero_state, running + state_grads[position])
    leaving = carried_in(running, opens, True)
    suffix = jnp.stack(suffix_list) + jnp.where(
        reach_right[:, None, None, None], leaving[None], 0.0
    )
    suffix_half = suffix.astype(jnp.bfloat16)
    kfeat_grad = jnp.einsum(
        "bshf,bhef->bshe", value_blocks, suffix_half, preferred_element_type=jnp.float32
    )
    kfeat_grad = (kfeat_grad + kfeat_inner).astype(jnp.bfloat16)
    value_grad = jnp.einsum(
        "bshe,bhef->bshf", kfeat, suffix_half, preferred_element_type=jnp.float32
    )
    value_grad = (
        value_grad
        + jnp.einsum("bhts,bthf->bshf", prob_half, grad_half, preferred_element_type=jnp.float32)
    ).astype(jnp.bfloat16)
    query_grad = jnp.einsum(
        "bthe,hde->bthd", qfeat_grad, weight_local, preferred_element_type=jnp.float32
    ).astype(jnp.bfloat16)
    key_grad = jnp.einsum(
        "bthe,hde->bthd", kfeat_grad, weight_local, preferred_element_type=jnp.float32
    ).astype(jnp.bfloat16)
    factor = (lax.axis_size("seq") * tokens_here) ** (-0.5)
    flat_shape = (tokens_here, head_count * HS)
    return (
        mixed.reshape(flat_shape),
        query_grad.reshape(flat_shape),
        key_grad.reshape(flat_shape),
        value_grad.reshape(flat_shape),
        owned_grad * factor,
        gain_sum * factor,
    )


def solution(mesh):
    placed = (
        P("seq", "fsdp"),
        P("seq", "fsdp"),
        P("seq", "fsdp"),
        P(None, "fsdp", "seq"),
        P("fsdp", None),
        P(),
        P("seq", "fsdp"),
    )
    return jax.shard_map(
        local,
        mesh=mesh,
        in_specs=placed,
        out_specs=(
            P("seq", "fsdp"),
            P("seq", "fsdp"),
            P("seq", "fsdp"),
            P("seq", "fsdp"),
            P(None, "fsdp", "seq"),
            P("fsdp", None),
        ),
        check_vma=False,
    )
```

```python
import jax
import jax.numpy as jnp
from jax import lax
from jax.sharding import PartitionSpec as P

HS = 128
BLK = 128


epsilon = 1.0
HIGH = lax.Precision.HIGHEST


def shifted(x, dist, backward):
    count = lax.axis_size("seq")
    if backward:
        pairs = [(i, i - dist) for i in range(dist, count)]
    else:
        pairs = [(i, i + dist) for i in range(count - dist)]
    return lax.ppermute(x, "seq", pairs)


def carried_in(aggregate, opens, backward):
    count = lax.axis_size("seq")
    place = lax.axis_index("seq")
    sign = 1 if backward else -1
    near = shifted(aggregate, 1, backward)
    far = shifted(aggregate, 2, backward)
    one = place + sign
    state = jnp.where(opens(one, one), near, far + near)
    covered = 2
    while covered < count:
        far = shifted(state, covered, backward)
        lo, hi = (place + 1, place + covered) if backward else (place - covered, place - 1)
        state = jnp.where(opens(lo, hi), state, far + state)
        covered *= 2
    return state


def project(rows, weight):
    return jnp.einsum("bthd,hde->bthe", rows, weight, preferred_element_type=jnp.float32).astype(
        jnp.bfloat16
    )


def local(queries, keys, values, feature_weight, norm_gain, doc_bounds, out_grad):
    head_groups = lax.all_to_all(feature_weight, "fsdp", split_axis=0, concat_axis=1, tiled=True)
    gathered = lax.all_gather(head_groups, "seq")
    head_count, rows, _ = head_groups.shape
    weight_local = gathered.transpose(1, 2, 0, 3).reshape(head_count, rows, -1)
    tokens_here = queries.shape[0]
    block_count = tokens_here // BLK
    block_shape = (block_count, BLK, head_count, HS)
    query_blocks = queries.reshape(block_shape)
    key_blocks = keys.reshape(block_shape)
    value_blocks = values.reshape(block_shape)

    place = lax.axis_index("seq")
    starts = doc_bounds[:, 0]
    start_device = starts // block_count

    def opens(lo, hi):
        return jnp.any((start_device >= lo) & (start_device <= hi))

    block_ids = place * block_count + jnp.arange(block_count, dtype=jnp.int32)
    starts_here = jnp.any(starts[None, :] == block_ids[:, None], axis=1)
    opened = jnp.cumsum(starts_here.astype(jnp.int32))
    reach_left = opened == 0
    reach_right = opened[-1] - opened == 0

    raw_updates = jnp.einsum(
        "bthd,bthf->bhdf", key_blocks, value_blocks, preferred_element_type=jnp.float32
    )
    zero_state = jnp.zeros(raw_updates.shape[1:], jnp.float32)
    running = zero_state
    prefix_list = []
    for position in range(block_count):
        held = jnp.where(starts_here[position], zero_state, running)
        prefix_list.append(held)
        running = held + raw_updates[position]
    entering = carried_in(running, opens, False)
    raw_states = jnp.stack(prefix_list) + jnp.where(
        reach_left[:, None, None, None], entering[None], 0.0
    )

    qfeat = project(query_blocks, weight_local)
    kfeat = project(key_blocks, weight_local)
    weight_f = weight_local.astype(jnp.float32)
    states = jnp.einsum("hde,bhdf->bhef", weight_f, raw_states, precision=HIGH)
    state_half = states.astype(jnp.bfloat16)
    causal = jnp.arange(BLK)[:, None] >= jnp.arange(BLK)[None, :]
    scores = jnp.einsum("bthe,bshe->bhts", qfeat, kfeat, preferred_element_type=jnp.float32)
    prob_half = jnp.where(causal, scores, 0.0).astype(jnp.bfloat16)
    mixed_f = jnp.einsum("bthe,bhef->bthf", qfeat, state_half, preferred_element_type=jnp.float32)
    mixed_f = mixed_f + jnp.einsum(
        "bhts,bshf->bthf", prob_half, value_blocks, preferred_element_type=jnp.float32
    )
    gains = norm_gain.astype(jnp.float32)
    inverse = lax.rsqrt(jnp.mean(mixed_f * mixed_f, axis=-1, keepdims=True) + epsilon)
    mixed = (mixed_f * inverse * gains).astype(jnp.bfloat16)
    grad_y = out_grad.reshape(block_shape).astype(jnp.float32)
    scaled = grad_y * gains
    grad_mix = inverse * (
        scaled - mixed_f * inverse * inverse * jnp.mean(scaled * mixed_f, axis=-1, keepdims=True)
    )
    grad_half = grad_mix.astype(jnp.bfloat16)
    gain_part = jnp.sum(grad_y * mixed_f * inverse, axis=(0, 1))

    state_grads = jnp.einsum(
        "bthe,bthf->bhef", qfeat, grad_half, preferred_element_type=jnp.float32
    )
    dot_grads = jnp.einsum(
        "bthf,bshf->bhts", grad_half, value_blocks, preferred_element_type=jnp.float32
    )
    dot_half = jnp.where(causal, dot_grads, 0.0).astype(jnp.bfloat16)
    qfeat_grad = jnp.einsum(
        "bthf,bhef->bthe", grad_half, state_half, preferred_element_type=jnp.float32
    )
    qfeat_grad = (
        qfeat_grad
        + jnp.einsum("bhts,bshe->bthe", dot_half, kfeat, preferred_element_type=jnp.float32)
    ).astype(jnp.bfloat16)
    kfeat_inner = jnp.einsum(
        "bhts,bthe->bshe", dot_half, qfeat, preferred_element_type=jnp.float32
    )
    weight_part = jnp.einsum(
        "bthd,bthe->hde", query_blocks, qfeat_grad, preferred_element_type=jnp.float32
    )
    weight_part = weight_part + jnp.einsum(
        "bthd,bthe->hde", key_blocks, kfeat_inner.astype(jnp.bfloat16),
        preferred_element_type=jnp.float32,
    )
    weight_part = weight_part + jnp.einsum(
        "bhdf,bhef->hde", raw_states, state_grads, precision=HIGH
    )
    summed = lax.psum(jnp.concatenate([weight_part, gain_part[:, None, :]], axis=1), "seq")
    gain_sum = summed[:, HS, :]
    column_width = HS // lax.axis_size("seq")
    weight_columns = lax.dynamic_slice_in_dim(
        summed[:, :HS, :], lax.axis_index("seq") * column_width, column_width, 2
    )
    owned_grad = lax.all_to_all(weight_columns, "fsdp", split_axis=1, concat_axis=0, tiled=True)

    running = zero_state
    suffix_list = [zero_state] * block_count
    for position in reversed(range(block_count)):
        suffix_list[position] = running
        running = jnp.where(starts_here[position], zero_state, running + state_grads[position])
    leaving = carried_in(running, opens, True)
    suffix = jnp.stack(suffix_list) + jnp.where(
        reach_right[:, None, None, None], leaving[None], 0.0
    )
    suffix_half = suffix.astype(jnp.bfloat16)
    kfeat_grad = jnp.einsum(
        "bshf,bhef->bshe", value_blocks, suffix_half, preferred_element_type=jnp.float32
    )
    kfeat_grad = (kfeat_grad + kfeat_inner).astype(jnp.bfloat16)
    value_grad = jnp.einsum(
        "bshe,bhef->bshf", kfeat, suffix_half, preferred_element_type=jnp.float32
    )
    value_grad = (
        value_grad
        + jnp.einsum("bhts,bthf->bshf", prob_half, grad_half, preferred_element_type=jnp.float32)
    ).astype(jnp.bfloat16)
    query_grad = jnp.einsum(
        "bthe,hde->bthd", qfeat_grad, weight_local, preferred_element_type=jnp.float32
    ).astype(jnp.bfloat16)
    key_grad = jnp.einsum(
        "bthe,hde->bthd", kfeat_grad, weight_local, preferred_element_type=jnp.float32
    ).astype(jnp.bfloat16)
    factor = (lax.axis_size("seq") * tokens_here) ** (-0.5)
    flat_shape = (tokens_here, head_count * HS)
    return (
        mixed.reshape(flat_shape),
        query_grad.reshape(flat_shape),
        key_grad.reshape(flat_shape),
        value_grad.reshape(flat_shape),
        owned_grad * factor,
        gain_sum * factor,
    )


def solution(mesh):
    placed = (
        P("seq", "fsdp"),
        P("seq", "fsdp"),
        P("seq", "fsdp"),
        P(None, "fsdp", "seq"),
        P("fsdp", None),
        P(),
        P("seq", "fsdp"),
    )
    return jax.shard_map(
        local,
        mesh=mesh,
        in_specs=placed,
        out_specs=(
            P("seq", "fsdp"),
            P("seq", "fsdp"),
            P("seq", "fsdp"),
            P("seq", "fsdp"),
            P(None, "fsdp", "seq"),
            P("fsdp", None),
        ),
        check_vma=False,
    )
```

```python
import jax
import jax.numpy as jnp
from jax import lax
from jax.sharding import PartitionSpec as P

HS = 128
BLK = 128


epsilon = 1.0
HIGH = lax.Precision.HIGHEST


def shifted(x, dist, backward):
    count = lax.axis_size("seq")
    if backward:
        pairs = [(i, i - dist) for i in range(dist, count)]
    else:
        pairs = [(i, i + dist) for i in range(count - dist)]
    return lax.ppermute(x, "seq", pairs)


def carried_in(aggregate, opens, backward):
    count = lax.axis_size("seq")
    place = lax.axis_index("seq")
    sign = 1 if backward else -1
    near = shifted(aggregate, 1, backward)
    far = shifted(aggregate, 2, backward)
    one = place + sign
    state = jnp.where(opens(one, one), near, far + near)
    covered = 2
    while covered < count:
        far = shifted(state, covered, backward)
        lo, hi = (place + 1, place + covered) if backward else (place - covered, place - 1)
        state = jnp.where(opens(lo, hi), state, far + state)
        covered *= 2
    return state


def project(rows, weight):
    return jnp.einsum("bthd,hde->bthe", rows, weight, preferred_element_type=jnp.float32).astype(
        jnp.bfloat16
    )


def local(queries, keys, values, feature_weight, norm_gain, doc_bounds, out_grad):
    seq_count = lax.axis_size("seq")
    fsdp_count = lax.axis_size("fsdp")
    all_heads, rows, columns = feature_weight.shape
    head_count = all_heads // fsdp_count
    gathered = lax.all_gather(feature_weight, ("seq", "fsdp"))
    weight_full = (
        gathered.reshape(seq_count, fsdp_count, all_heads, rows, columns)
        .transpose(2, 1, 3, 0, 4)
        .reshape(all_heads, rows * fsdp_count, columns * seq_count)
    )
    group = lax.axis_index("fsdp")
    weight_local = lax.dynamic_slice_in_dim(weight_full, group * head_count, head_count, 0)
    tokens_here = queries.shape[0]
    block_count = tokens_here // BLK
    block_shape = (block_count, BLK, head_count, HS)
    query_blocks = queries.reshape(block_shape)
    key_blocks = keys.reshape(block_shape)
    value_blocks = values.reshape(block_shape)

    place = lax.axis_index("seq")
    starts = doc_bounds[:, 0]
    start_device = starts // block_count

    def opens(lo, hi):
        return jnp.any((start_device >= lo) & (start_device <= hi))

    block_ids = place * block_count + jnp.arange(block_count, dtype=jnp.int32)
    starts_here = jnp.any(starts[None, :] == block_ids[:, None], axis=1)
    opened = jnp.cumsum(starts_here.astype(jnp.int32))
    reach_left = opened == 0
    reach_right = opened[-1] - opened == 0

    raw_updates = jnp.einsum(
        "bthd,bthf->bhdf", key_blocks, value_blocks, preferred_element_type=jnp.float32
    )
    zero_state = jnp.zeros(raw_updates.shape[1:], jnp.float32)
    running = zero_state
    prefix_list = []
    for position in range(block_count):
        held = jnp.where(starts_here[position], zero_state, running)
        prefix_list.append(held)
        running = held + raw_updates[position]
    entering = carried_in(running, opens, False)
    raw_states = jnp.stack(prefix_list) + jnp.where(
        reach_left[:, None, None, None], entering[None], 0.0
    )

    qfeat = project(query_blocks, weight_local)
    kfeat = project(key_blocks, weight_local)
    weight_f = weight_local.astype(jnp.float32)
    states = jnp.einsum("hde,bhdf->bhef", weight_f, raw_states, precision=HIGH)
    state_half = states.astype(jnp.bfloat16)
    causal = jnp.arange(BLK)[:, None] >= jnp.arange(BLK)[None, :]
    scores = jnp.einsum("bthe,bshe->bhts", qfeat, kfeat, preferred_element_type=jnp.float32)
    prob_half = jnp.where(causal, scores, 0.0).astype(jnp.bfloat16)
    mixed_f = jnp.einsum("bthe,bhef->bthf", qfeat, state_half, preferred_element_type=jnp.float32)
    mixed_f = mixed_f + jnp.einsum(
        "bhts,bshf->bthf", prob_half, value_blocks, preferred_element_type=jnp.float32
    )
    gains = norm_gain.astype(jnp.float32)
    inverse = lax.rsqrt(jnp.mean(mixed_f * mixed_f, axis=-1, keepdims=True) + epsilon)
    mixed = (mixed_f * inverse * gains).astype(jnp.bfloat16)
    grad_y = out_grad.reshape(block_shape).astype(jnp.float32)
    scaled = grad_y * gains
    grad_mix = inverse * (
        scaled - mixed_f * inverse * inverse * jnp.mean(scaled * mixed_f, axis=-1, keepdims=True)
    )
    grad_half = grad_mix.astype(jnp.bfloat16)
    gain_part = jnp.sum(grad_y * mixed_f * inverse, axis=(0, 1))

    state_grads = jnp.einsum(
        "bthe,bthf->bhef", qfeat, grad_half, preferred_element_type=jnp.float32
    )
    dot_grads = jnp.einsum(
        "bthf,bshf->bhts", grad_half, value_blocks, preferred_element_type=jnp.float32
    )
    dot_half = jnp.where(causal, dot_grads, 0.0).astype(jnp.bfloat16)
    qfeat_grad = jnp.einsum(
        "bthf,bhef->bthe", grad_half, state_half, preferred_element_type=jnp.float32
    )
    qfeat_grad = (
        qfeat_grad
        + jnp.einsum("bhts,bshe->bthe", dot_half, kfeat, preferred_element_type=jnp.float32)
    ).astype(jnp.bfloat16)
    kfeat_inner = jnp.einsum(
        "bhts,bthe->bshe", dot_half, qfeat, preferred_element_type=jnp.float32
    )
    weight_part = jnp.einsum(
        "bthd,bthe->hde", query_blocks, qfeat_grad, preferred_element_type=jnp.float32
    )
    weight_part = weight_part + jnp.einsum(
        "bthd,bthe->hde", key_blocks, kfeat_inner.astype(jnp.bfloat16),
        preferred_element_type=jnp.float32,
    )
    weight_part = weight_part + jnp.einsum(
        "bhdf,bhef->hde", raw_states, state_grads, precision=HIGH
    )
    own_slot = jnp.concatenate([weight_part, gain_part[:, None, :]], axis=1)
    slots = jnp.zeros((all_heads,) + own_slot.shape[1:], jnp.float32)
    slots = lax.dynamic_update_slice_in_dim(slots, own_slot, group * head_count, 0)
    summed = lax.psum(slots, ("seq", "fsdp"))
    gain_sum = lax.dynamic_slice_in_dim(summed[:, HS, :], group * head_count, head_count, 0)
    owned_grad = lax.dynamic_slice(
        summed, (0, group * rows, place * columns), (all_heads, rows, columns)
    )

    running = zero_state
    suffix_list = [zero_state] * block_count
    for position in reversed(range(block_count)):
        suffix_list[position] = running
        running = jnp.where(starts_here[position], zero_state, running + state_grads[position])
    leaving = carried_in(running, opens, True)
    suffix = jnp.stack(suffix_list) + jnp.where(
        reach_right[:, None, None, None], leaving[None], 0.0
    )
    suffix_half = suffix.astype(jnp.bfloat16)
    kfeat_grad = jnp.einsum(
        "bshf,bhef->bshe", value_blocks, suffix_half, preferred_element_type=jnp.float32
    )
    kfeat_grad = (kfeat_grad + kfeat_inner).astype(jnp.bfloat16)
    value_grad = jnp.einsum(
        "bshe,bhef->bshf", kfeat, suffix_half, preferred_element_type=jnp.float32
    )
    value_grad = (
        value_grad
        + jnp.einsum("bhts,bthf->bshf", prob_half, grad_half, preferred_element_type=jnp.float32)
    ).astype(jnp.bfloat16)
    query_grad = jnp.einsum(
        "bthe,hde->bthd", qfeat_grad, weight_local, preferred_element_type=jnp.float32
    ).astype(jnp.bfloat16)
    key_grad = jnp.einsum(
        "bthe,hde->bthd", kfeat_grad, weight_local, preferred_element_type=jnp.float32
    ).astype(jnp.bfloat16)
    factor = (lax.axis_size("seq") * tokens_here) ** (-0.5)
    flat_shape = (tokens_here, head_count * HS)
    return (
        mixed.reshape(flat_shape),
        query_grad.reshape(flat_shape),
        key_grad.reshape(flat_shape),
        value_grad.reshape(flat_shape),
        owned_grad * factor,
        gain_sum * factor,
    )


def solution(mesh):
    placed = (
        P("seq", "fsdp"),
        P("seq", "fsdp"),
        P("seq", "fsdp"),
        P(None, "fsdp", "seq"),
        P("fsdp", None),
        P(),
        P("seq", "fsdp"),
    )
    return jax.shard_map(
        local,
        mesh=mesh,
        in_specs=placed,
        out_specs=(
            P("seq", "fsdp"),
            P("seq", "fsdp"),
            P("seq", "fsdp"),
            P("seq", "fsdp"),
            P(None, "fsdp", "seq"),
            P("fsdp", None),
        ),
        check_vma=False,
    )
```

```python
import jax
import jax.numpy as jnp
from jax import lax
from jax.sharding import PartitionSpec as P

HS = 128
BLK = 128


epsilon = 1.0
HIGH = lax.Precision.HIGHEST


def shifted(x, dist, backward):
    count = lax.axis_size("seq")
    if backward:
        pairs = [(i, i - dist) for i in range(dist, count)]
    else:
        pairs = [(i, i + dist) for i in range(count - dist)]
    return lax.ppermute(x, "seq", pairs)


def carried_in(aggregate, opens, backward):
    count = lax.axis_size("seq")
    place = lax.axis_index("seq")
    sign = 1 if backward else -1
    near = shifted(aggregate, 1, backward)
    far = shifted(aggregate, 2, backward)
    one = place + sign
    state = jnp.where(opens(one, one), near, far + near)
    covered = 2
    while covered < count:
        far = shifted(state, covered, backward)
        lo, hi = (place + 1, place + covered) if backward else (place - covered, place - 1)
        state = jnp.where(opens(lo, hi), state, far + state)
        covered *= 2
    return state


def exchanged(x, bit):
    count = lax.axis_size("seq")
    return lax.ppermute(x, "seq", [(i, i ^ bit) for i in range(count)])


def gathered_columns(piece):
    count = lax.axis_size("seq")
    place = lax.axis_index("seq")
    bit = 1
    while bit < count:
        other = exchanged(piece, bit)
        upper = (place & bit) > 0
        piece = jnp.where(
            upper, jnp.concatenate([other, piece], -1), jnp.concatenate([piece, other], -1)
        )
        bit *= 2
    return piece


def summed_columns(part, extra):
    count = lax.axis_size("seq")
    place = lax.axis_index("seq")
    bit = count // 2
    while bit >= 1:
        half = part.shape[-1] // 2
        low, high = part[..., :half], part[..., half:]
        upper = (place & bit) > 0
        kept = jnp.where(upper, high, low)
        sent = jnp.where(upper, low, high)
        got = exchanged(jnp.concatenate([sent, extra[..., None]], -1), bit)
        part = kept + got[..., :half]
        extra = extra + got[..., half]
        bit //= 2
    return part, extra


def project(rows, weight):
    return jnp.einsum("bthd,hde->bthe", rows, weight, preferred_element_type=jnp.float32).astype(
        jnp.bfloat16
    )


def local(queries, keys, values, feature_weight, norm_gain, doc_bounds, out_grad):
    head_groups = lax.all_to_all(feature_weight, "fsdp", split_axis=0, concat_axis=1, tiled=True)
    weight_local = gathered_columns(head_groups)
    head_count = weight_local.shape[0]
    tokens_here = queries.shape[0]
    block_count = tokens_here // BLK
    block_shape = (block_count, BLK, head_count, HS)
    query_blocks = queries.reshape(block_shape)
    key_blocks = keys.reshape(block_shape)
    value_blocks = values.reshape(block_shape)

    place = lax.axis_index("seq")
    starts = doc_bounds[:, 0]
    start_device = starts // block_count

    def opens(lo, hi):
        return jnp.any((start_device >= lo) & (start_device <= hi))

    block_ids = place * block_count + jnp.arange(block_count, dtype=jnp.int32)
    starts_here = jnp.any(starts[None, :] == block_ids[:, None], axis=1)
    opened = jnp.cumsum(starts_here.astype(jnp.int32))
    reach_left = opened == 0
    reach_right = opened[-1] - opened == 0

    raw_updates = jnp.einsum(
        "bthd,bthf->bhdf", key_blocks, value_blocks, preferred_element_type=jnp.float32
    )
    zero_state = jnp.zeros(raw_updates.shape[1:], jnp.float32)
    running = zero_state
    prefix_list = []
    for position in range(block_count):
        held = jnp.where(starts_here[position], zero_state, running)
        prefix_list.append(held)
        running = held + raw_updates[position]
    entering = carried_in(running, opens, False)
    raw_states = jnp.stack(prefix_list) + jnp.where(
        reach_left[:, None, None, None], entering[None], 0.0
    )

    qfeat = project(query_blocks, weight_local)
    kfeat = project(key_blocks, weight_local)
    weight_f = weight_local.astype(jnp.float32)
    states = jnp.einsum("hde,bhdf->bhef", weight_f, raw_states, precision=HIGH)
    state_half = states.astype(jnp.bfloat16)
    causal = jnp.arange(BLK)[:, None] >= jnp.arange(BLK)[None, :]
    scores = jnp.einsum("bthe,bshe->bhts", qfeat, kfeat, preferred_element_type=jnp.float32)
    prob_half = jnp.where(causal, scores, 0.0).astype(jnp.bfloat16)
    mixed_f = jnp.einsum("bthe,bhef->bthf", qfeat, state_half, preferred_element_type=jnp.float32)
    mixed_f = mixed_f + jnp.einsum(
        "bhts,bshf->bthf", prob_half, value_blocks, preferred_element_type=jnp.float32
    )
    gains = norm_gain.astype(jnp.float32)
    inverse = lax.rsqrt(jnp.mean(mixed_f * mixed_f, axis=-1, keepdims=True) + epsilon)
    mixed = (mixed_f * inverse * gains).astype(jnp.bfloat16)
    grad_y = out_grad.reshape(block_shape).astype(jnp.float32)
    scaled = grad_y * gains
    grad_mix = inverse * (
        scaled - mixed_f * inverse * inverse * jnp.mean(scaled * mixed_f, axis=-1, keepdims=True)
    )
    grad_half = grad_mix.astype(jnp.bfloat16)
    gain_part = jnp.sum(grad_y * mixed_f * inverse, axis=(0, 1))

    state_grads = jnp.einsum(
        "bthe,bthf->bhef", qfeat, grad_half, preferred_element_type=jnp.float32
    )
    dot_grads = jnp.einsum(
        "bthf,bshf->bhts", grad_half, value_blocks, preferred_element_type=jnp.float32
    )
    dot_half = jnp.where(causal, dot_grads, 0.0).astype(jnp.bfloat16)
    qfeat_grad = jnp.einsum(
        "bthf,bhef->bthe", grad_half, state_half, preferred_element_type=jnp.float32
    )
    qfeat_grad = (
        qfeat_grad
        + jnp.einsum("bhts,bshe->bthe", dot_half, kfeat, preferred_element_type=jnp.float32)
    ).astype(jnp.bfloat16)
    kfeat_inner = jnp.einsum(
        "bhts,bthe->bshe", dot_half, qfeat, preferred_element_type=jnp.float32
    )
    weight_part = jnp.einsum(
        "bthd,bthe->hde", query_blocks, qfeat_grad, preferred_element_type=jnp.float32
    )
    weight_part = weight_part + jnp.einsum(
        "bthd,bthe->hde", key_blocks, kfeat_inner.astype(jnp.bfloat16),
        preferred_element_type=jnp.float32,
    )
    weight_part = weight_part + jnp.einsum(
        "bhdf,bhef->hde", raw_states, state_grads, precision=HIGH
    )
    weight_columns, gain_sum = summed_columns(weight_part, gain_part)
    owned_grad = lax.all_to_all(weight_columns, "fsdp", split_axis=1, concat_axis=0, tiled=True)

    running = zero_state
    suffix_list = [zero_state] * block_count
    for position in reversed(range(block_count)):
        suffix_list[position] = running
        running = jnp.where(starts_here[position], zero_state, running + state_grads[position])
    leaving = carried_in(running, opens, True)
    suffix = jnp.stack(suffix_list) + jnp.where(
        reach_right[:, None, None, None], leaving[None], 0.0
    )
    suffix_half = suffix.astype(jnp.bfloat16)
    kfeat_grad = jnp.einsum(
        "bshf,bhef->bshe", value_blocks, suffix_half, preferred_element_type=jnp.float32
    )
    kfeat_grad = (kfeat_grad + kfeat_inner).astype(jnp.bfloat16)
    value_grad = jnp.einsum(
        "bshe,bhef->bshf", kfeat, suffix_half, preferred_element_type=jnp.float32
    )
    value_grad = (
        value_grad
        + jnp.einsum("bhts,bthf->bshf", prob_half, grad_half, preferred_element_type=jnp.float32)
    ).astype(jnp.bfloat16)
    query_grad = jnp.einsum(
        "bthe,hde->bthd", qfeat_grad, weight_local, preferred_element_type=jnp.float32
    ).astype(jnp.bfloat16)
    key_grad = jnp.einsum(
        "bthe,hde->bthd", kfeat_grad, weight_local, preferred_element_type=jnp.float32
    ).astype(jnp.bfloat16)
    factor = (lax.axis_size("seq") * tokens_here) ** (-0.5)
    flat_shape = (tokens_here, head_count * HS)
    return (
        mixed.reshape(flat_shape),
        query_grad.reshape(flat_shape),
        key_grad.reshape(flat_shape),
        value_grad.reshape(flat_shape),
        owned_grad * factor,
        gain_sum * factor,
    )


def solution(mesh):
    placed = (
        P("seq", "fsdp"),
        P("seq", "fsdp"),
        P("seq", "fsdp"),
        P(None, "fsdp", "seq"),
        P("fsdp", None),
        P(),
        P("seq", "fsdp"),
    )
    return jax.shard_map(
        local,
        mesh=mesh,
        in_specs=placed,
        out_specs=(
            P("seq", "fsdp"),
            P("seq", "fsdp"),
            P("seq", "fsdp"),
            P("seq", "fsdp"),
            P(None, "fsdp", "seq"),
            P("fsdp", None),
        ),
        check_vma=False,
    )
```

```python
import jax
import jax.numpy as jnp
from jax import lax
from jax.sharding import PartitionSpec as P

HS = 128
BLK = 128


epsilon = 1.0
HIGH = lax.Precision.HIGHEST


RADIX = 4


def shifted(x, dist, backward):
    count = lax.axis_size("seq")
    if dist >= count:
        return jnp.zeros_like(x)
    if backward:
        pairs = [(i, i - dist) for i in range(dist, count)]
    else:
        pairs = [(i, i + dist) for i in range(count - dist)]
    return lax.ppermute(x, "seq", pairs)


def carried_in(aggregate, opens, backward):
    count = lax.axis_size("seq")
    place = lax.axis_index("seq")
    sign = 1 if backward else -1

    def span(dist, width):
        first = place + sign * dist
        last = place + sign * (dist + width - 1)
        return (last, first) if sign < 0 else (first, last)

    pieces = [shifted(aggregate, m, backward) for m in range(1, RADIX + 1)]
    state = pieces[-1]
    for m in range(RADIX - 1, 0, -1):
        state = jnp.where(opens(*span(m, 1)), pieces[m - 1], state + pieces[m - 1])
    covered = RADIX
    while covered < count:
        pieces = [shifted(state, m * covered, backward) for m in range(1, RADIX)]
        merged = pieces[-1]
        for m in range(RADIX - 2, 0, -1):
            merged = jnp.where(opens(*span(m * covered + 1, covered)), pieces[m - 1], merged + pieces[m - 1])
        state = jnp.where(opens(*span(1, covered)), state, merged + state)
        covered *= RADIX
    return state


def exchanged(x, mask):
    count = lax.axis_size("seq")
    return lax.ppermute(x, "seq", [(i, i ^ mask) for i in range(count)])


def gathered_columns(piece):
    count = lax.axis_size("seq")
    place = lax.axis_index("seq")
    base = 1
    while base < count:
        digit = (place // base) % RADIX
        got = [piece] + [exchanged(piece, m * base) for m in range(1, RADIX)]
        piece = jnp.concatenate(
            [lax.select_n(digit ^ v, *got) for v in range(RADIX)], -1
        )
        base *= RADIX
    return piece


def summed_columns(part, extra):
    count = lax.axis_size("seq")
    place = lax.axis_index("seq")
    base = count // RADIX
    while base >= 1:
        width = part.shape[-1] // RADIX
        quarters = [part[..., v * width:(v + 1) * width] for v in range(RADIX)]
        digit = (place // base) % RADIX
        part = lax.select_n(digit, *quarters)
        total = extra
        for m in range(1, RADIX):
            sent = lax.select_n(digit ^ m, *quarters)
            got = exchanged(jnp.concatenate([sent, extra[..., None]], -1), m * base)
            part = part + got[..., :width]
            total = total + got[..., width]
        extra = total
        base //= RADIX
    return part, extra


def project(rows, weight):
    return jnp.einsum("bthd,hde->bthe", rows, weight, preferred_element_type=jnp.float32).astype(
        jnp.bfloat16
    )


def local(queries, keys, values, feature_weight, norm_gain, doc_bounds, out_grad):
    head_groups = lax.all_to_all(feature_weight, "fsdp", split_axis=0, concat_axis=1, tiled=True)
    weight_local = gathered_columns(head_groups)
    head_count = weight_local.shape[0]
    tokens_here = queries.shape[0]
    block_count = tokens_here // BLK
    block_shape = (block_count, BLK, head_count, HS)
    query_blocks = queries.reshape(block_shape)
    key_blocks = keys.reshape(block_shape)
    value_blocks = values.reshape(block_shape)

    place = lax.axis_index("seq")
    starts = doc_bounds[:, 0]
    start_device = starts // block_count

    def opens(lo, hi):
        return jnp.any((start_device >= lo) & (start_device <= hi))

    block_ids = place * block_count + jnp.arange(block_count, dtype=jnp.int32)
    starts_here = jnp.any(starts[None, :] == block_ids[:, None], axis=1)
    opened = jnp.cumsum(starts_here.astype(jnp.int32))
    reach_left = opened == 0
    reach_right = opened[-1] - opened == 0

    raw_updates = jnp.einsum(
        "bthd,bthf->bhdf", key_blocks, value_blocks, preferred_element_type=jnp.float32
    )
    zero_state = jnp.zeros(raw_updates.shape[1:], jnp.float32)
    running = zero_state
    prefix_list = []
    for position in range(block_count):
        held = jnp.where(starts_here[position], zero_state, running)
        prefix_list.append(held)
        running = held + raw_updates[position]
    entering = carried_in(running, opens, False)
    raw_states = jnp.stack(prefix_list) + jnp.where(
        reach_left[:, None, None, None], entering[None], 0.0
    )

    qfeat = project(query_blocks, weight_local)
    kfeat = project(key_blocks, weight_local)
    weight_f = weight_local.astype(jnp.float32)
    states = jnp.einsum("hde,bhdf->bhef", weight_f, raw_states, precision=HIGH)
    state_half = states.astype(jnp.bfloat16)
    causal = jnp.arange(BLK)[:, None] >= jnp.arange(BLK)[None, :]
    scores = jnp.einsum("bthe,bshe->bhts", qfeat, kfeat, preferred_element_type=jnp.float32)
    prob_half = jnp.where(causal, scores, 0.0).astype(jnp.bfloat16)
    mixed_f = jnp.einsum("bthe,bhef->bthf", qfeat, state_half, preferred_element_type=jnp.float32)
    mixed_f = mixed_f + jnp.einsum(
        "bhts,bshf->bthf", prob_half, value_blocks, preferred_element_type=jnp.float32
    )
    gains = norm_gain.astype(jnp.float32)
    inverse = lax.rsqrt(jnp.mean(mixed_f * mixed_f, axis=-1, keepdims=True) + epsilon)
    mixed = (mixed_f * inverse * gains).astype(jnp.bfloat16)
    grad_y = out_grad.reshape(block_shape).astype(jnp.float32)
    scaled = grad_y * gains
    grad_mix = inverse * (
        scaled - mixed_f * inverse * inverse * jnp.mean(scaled * mixed_f, axis=-1, keepdims=True)
    )
    grad_half = grad_mix.astype(jnp.bfloat16)
    gain_part = jnp.sum(grad_y * mixed_f * inverse, axis=(0, 1))

    state_grads = jnp.einsum(
        "bthe,bthf->bhef", qfeat, grad_half, preferred_element_type=jnp.float32
    )
    dot_grads = jnp.einsum(
        "bthf,bshf->bhts", grad_half, value_blocks, preferred_element_type=jnp.float32
    )
    dot_half = jnp.where(causal, dot_grads, 0.0).astype(jnp.bfloat16)
    qfeat_grad = jnp.einsum(
        "bthf,bhef->bthe", grad_half, state_half, preferred_element_type=jnp.float32
    )
    qfeat_grad = (
        qfeat_grad
        + jnp.einsum("bhts,bshe->bthe", dot_half, kfeat, preferred_element_type=jnp.float32)
    ).astype(jnp.bfloat16)
    kfeat_inner = jnp.einsum(
        "bhts,bthe->bshe", dot_half, qfeat, preferred_element_type=jnp.float32
    )
    weight_part = jnp.einsum(
        "bthd,bthe->hde", query_blocks, qfeat_grad, preferred_element_type=jnp.float32
    )
    weight_part = weight_part + jnp.einsum(
        "bthd,bthe->hde", key_blocks, kfeat_inner.astype(jnp.bfloat16),
        preferred_element_type=jnp.float32,
    )
    weight_part = weight_part + jnp.einsum(
        "bhdf,bhef->hde", raw_states, state_grads, precision=HIGH
    )
    weight_columns, gain_sum = summed_columns(weight_part, gain_part)
    owned_grad = lax.all_to_all(weight_columns, "fsdp", split_axis=1, concat_axis=0, tiled=True)

    running = zero_state
    suffix_list = [zero_state] * block_count
    for position in reversed(range(block_count)):
        suffix_list[position] = running
        running = jnp.where(starts_here[position], zero_state, running + state_grads[position])
    leaving = carried_in(running, opens, True)
    suffix = jnp.stack(suffix_list) + jnp.where(
        reach_right[:, None, None, None], leaving[None], 0.0
    )
    suffix_half = suffix.astype(jnp.bfloat16)
    kfeat_grad = jnp.einsum(
        "bshf,bhef->bshe", value_blocks, suffix_half, preferred_element_type=jnp.float32
    )
    kfeat_grad = (kfeat_grad + kfeat_inner).astype(jnp.bfloat16)
    value_grad = jnp.einsum(
        "bshe,bhef->bshf", kfeat, suffix_half, preferred_element_type=jnp.float32
    )
    value_grad = (
        value_grad
        + jnp.einsum("bhts,bthf->bshf", prob_half, grad_half, preferred_element_type=jnp.float32)
    ).astype(jnp.bfloat16)
    query_grad = jnp.einsum(
        "bthe,hde->bthd", qfeat_grad, weight_local, preferred_element_type=jnp.float32
    ).astype(jnp.bfloat16)
    key_grad = jnp.einsum(
        "bthe,hde->bthd", kfeat_grad, weight_local, preferred_element_type=jnp.float32
    ).astype(jnp.bfloat16)
    factor = (lax.axis_size("seq") * tokens_here) ** (-0.5)
    flat_shape = (tokens_here, head_count * HS)
    return (
        mixed.reshape(flat_shape),
        query_grad.reshape(flat_shape),
        key_grad.reshape(flat_shape),
        value_grad.reshape(flat_shape),
        owned_grad * factor,
        gain_sum * factor,
    )


def solution(mesh):
    placed = (
        P("seq", "fsdp"),
        P("seq", "fsdp"),
        P("seq", "fsdp"),
        P(None, "fsdp", "seq"),
        P("fsdp", None),
        P(),
        P("seq", "fsdp"),
    )
    return jax.shard_map(
        local,
        mesh=mesh,
        in_specs=placed,
        out_specs=(
            P("seq", "fsdp"),
            P("seq", "fsdp"),
            P("seq", "fsdp"),
            P("seq", "fsdp"),
            P(None, "fsdp", "seq"),
            P("fsdp", None),
        ),
        check_vma=False,
    )
```

```python
import jax
import jax.numpy as jnp
from jax import lax
from jax.sharding import PartitionSpec as P

HS = 128
BLK = 128


epsilon = 1.0
HIGH = lax.Precision.HIGHEST
OUTER = "seq_row"
INNER = "seq_col"


def shifted(x, dist, backward):
    count = lax.axis_size((OUTER, INNER))
    if backward:
        pairs = [(i, i - dist) for i in range(dist, count)]
    else:
        pairs = [(i, i + dist) for i in range(count - dist)]
    return lax.ppermute(x, (OUTER, INNER), pairs)


def masked_sum(mask, stacked):
    return jnp.sum(jnp.where(mask[:, None, None, None], stacked, 0.0), 0)


def carried_in(aggregate, last_open, backward):
    inner = lax.axis_size(INNER)
    outer = lax.axis_size(OUTER)
    col = lax.axis_index(INNER)
    row = lax.axis_index(OUTER)
    place = row * inner + col
    near = place + 1 if backward else place - 1
    bound = last_open(near)
    cols = jnp.arange(inner)
    rows = jnp.arange(outer)
    in_row = lax.all_gather(aggregate, INNER)
    if backward:
        mine = (cols > col) & (row * inner + cols <= bound)
        row_bound = last_open(row * inner)
        carry = (row * inner + cols <= row_bound)
    else:
        mine = (cols < col) & (row * inner + cols >= bound)
        row_bound = last_open(row * inner + inner - 1)
        carry = (row * inner + cols >= row_bound)
    local_sum = masked_sum(mine, in_row)
    row_part = masked_sum(carry, in_row)
    across = lax.all_gather(row_part, OUTER)
    bound_row = bound // inner
    if backward:
        take = (rows > row) & (rows <= bound_row)
    else:
        take = (rows < row) & (rows >= bound_row)
    far_sum = masked_sum(take, across)
    return local_sum + far_sum


def exchanged(x, bit):
    count = lax.axis_size((OUTER, INNER))
    return lax.ppermute(x, (OUTER, INNER), [(i, i ^ bit) for i in range(count)])


def gathered_columns(piece):
    count = lax.axis_size((OUTER, INNER))
    place = lax.axis_index((OUTER, INNER))
    bit = 1
    while bit < count:
        other = exchanged(piece, bit)
        upper = (place & bit) > 0
        piece = jnp.where(
            upper, jnp.concatenate([other, piece], -1), jnp.concatenate([piece, other], -1)
        )
        bit *= 2
    return piece


def summed_columns(part, extra):
    count = lax.axis_size((OUTER, INNER))
    place = lax.axis_index((OUTER, INNER))
    bit = count // 2
    while bit >= 1:
        half = part.shape[-1] // 2
        low, high = part[..., :half], part[..., half:]
        upper = (place & bit) > 0
        kept = jnp.where(upper, high, low)
        sent = jnp.where(upper, low, high)
        got = exchanged(jnp.concatenate([sent, extra[..., None]], -1), bit)
        part = kept + got[..., :half]
        extra = extra + got[..., half]
        bit //= 2
    return part, extra


def project(rows, weight):
    return jnp.einsum("bthd,hde->bthe", rows, weight, preferred_element_type=jnp.float32).astype(
        jnp.bfloat16
    )


def local(queries, keys, values, feature_weight, norm_gain, doc_bounds, out_grad):
    head_groups = lax.all_to_all(feature_weight, "fsdp", split_axis=0, concat_axis=1, tiled=True)
    weight_local = gathered_columns(head_groups)
    head_count = weight_local.shape[0]
    tokens_here = queries.shape[0]
    block_count = tokens_here // BLK
    block_shape = (block_count, BLK, head_count, HS)
    query_blocks = queries.reshape(block_shape)
    key_blocks = keys.reshape(block_shape)
    value_blocks = values.reshape(block_shape)

    place = lax.axis_index((OUTER, INNER))
    starts = doc_bounds[:, 0]
    start_device = starts // block_count

    def last_open(device):
        return jnp.max(jnp.where(start_device <= device, start_device, 0))

    def next_open(device):
        count = lax.axis_size((OUTER, INNER))
        return jnp.min(jnp.where(start_device >= device, start_device, count - 1))

    block_ids = place * block_count + jnp.arange(block_count, dtype=jnp.int32)
    starts_here = jnp.any(starts[None, :] == block_ids[:, None], axis=1)
    opened = jnp.cumsum(starts_here.astype(jnp.int32))
    reach_left = opened == 0
    reach_right = opened[-1] - opened == 0

    raw_updates = jnp.einsum(
        "bthd,bthf->bhdf", key_blocks, value_blocks, preferred_element_type=jnp.float32
    )
    zero_state = jnp.zeros(raw_updates.shape[1:], jnp.float32)
    running = zero_state
    prefix_list = []
    for position in range(block_count):
        held = jnp.where(starts_here[position], zero_state, running)
        prefix_list.append(held)
        running = held + raw_updates[position]
    entering = carried_in(running, last_open, False)
    raw_states = jnp.stack(prefix_list) + jnp.where(
        reach_left[:, None, None, None], entering[None], 0.0
    )

    qfeat = project(query_blocks, weight_local)
    kfeat = project(key_blocks, weight_local)
    weight_f = weight_local.astype(jnp.float32)
    states = jnp.einsum("hde,bhdf->bhef", weight_f, raw_states, precision=HIGH)
    state_half = states.astype(jnp.bfloat16)
    causal = jnp.arange(BLK)[:, None] >= jnp.arange(BLK)[None, :]
    scores = jnp.einsum("bthe,bshe->bhts", qfeat, kfeat, preferred_element_type=jnp.float32)
    prob_half = jnp.where(causal, scores, 0.0).astype(jnp.bfloat16)
    mixed_f = jnp.einsum("bthe,bhef->bthf", qfeat, state_half, preferred_element_type=jnp.float32)
    mixed_f = mixed_f + jnp.einsum(
        "bhts,bshf->bthf", prob_half, value_blocks, preferred_element_type=jnp.float32
    )
    gains = norm_gain.astype(jnp.float32)
    inverse = lax.rsqrt(jnp.mean(mixed_f * mixed_f, axis=-1, keepdims=True) + epsilon)
    mixed = (mixed_f * inverse * gains).astype(jnp.bfloat16)
    grad_y = out_grad.reshape(block_shape).astype(jnp.float32)
    scaled = grad_y * gains
    grad_mix = inverse * (
        scaled - mixed_f * inverse * inverse * jnp.mean(scaled * mixed_f, axis=-1, keepdims=True)
    )
    grad_half = grad_mix.astype(jnp.bfloat16)
    gain_part = jnp.sum(grad_y * mixed_f * inverse, axis=(0, 1))

    state_grads = jnp.einsum(
        "bthe,bthf->bhef", qfeat, grad_half, preferred_element_type=jnp.float32
    )
    dot_grads = jnp.einsum(
        "bthf,bshf->bhts", grad_half, value_blocks, preferred_element_type=jnp.float32
    )
    dot_half = jnp.where(causal, dot_grads, 0.0).astype(jnp.bfloat16)
    qfeat_grad = jnp.einsum(
        "bthf,bhef->bthe", grad_half, state_half, preferred_element_type=jnp.float32
    )
    qfeat_grad = (
        qfeat_grad
        + jnp.einsum("bhts,bshe->bthe", dot_half, kfeat, preferred_element_type=jnp.float32)
    ).astype(jnp.bfloat16)
    kfeat_inner = jnp.einsum(
        "bhts,bthe->bshe", dot_half, qfeat, preferred_element_type=jnp.float32
    )
    weight_part = jnp.einsum(
        "bthd,bthe->hde", query_blocks, qfeat_grad, preferred_element_type=jnp.float32
    )
    weight_part = weight_part + jnp.einsum(
        "bthd,bthe->hde", key_blocks, kfeat_inner.astype(jnp.bfloat16),
        preferred_element_type=jnp.float32,
    )
    weight_part = weight_part + jnp.einsum(
        "bhdf,bhef->hde", raw_states, state_grads, precision=HIGH
    )
    weight_columns, gain_sum = summed_columns(weight_part, gain_part)
    owned_grad = lax.all_to_all(weight_columns, "fsdp", split_axis=1, concat_axis=0, tiled=True)

    running = zero_state
    suffix_list = [zero_state] * block_count
    for position in reversed(range(block_count)):
        suffix_list[position] = running
        running = jnp.where(starts_here[position], zero_state, running + state_grads[position])
    leaving = carried_in(running, next_open, True)
    suffix = jnp.stack(suffix_list) + jnp.where(
        reach_right[:, None, None, None], leaving[None], 0.0
    )
    suffix_half = suffix.astype(jnp.bfloat16)
    kfeat_grad = jnp.einsum(
        "bshf,bhef->bshe", value_blocks, suffix_half, preferred_element_type=jnp.float32
    )
    kfeat_grad = (kfeat_grad + kfeat_inner).astype(jnp.bfloat16)
    value_grad = jnp.einsum(
        "bshe,bhef->bshf", kfeat, suffix_half, preferred_element_type=jnp.float32
    )
    value_grad = (
        value_grad
        + jnp.einsum("bhts,bthf->bshf", prob_half, grad_half, preferred_element_type=jnp.float32)
    ).astype(jnp.bfloat16)
    query_grad = jnp.einsum(
        "bthe,hde->bthd", qfeat_grad, weight_local, preferred_element_type=jnp.float32
    ).astype(jnp.bfloat16)
    key_grad = jnp.einsum(
        "bthe,hde->bthd", kfeat_grad, weight_local, preferred_element_type=jnp.float32
    ).astype(jnp.bfloat16)
    factor = (lax.axis_size((OUTER, INNER)) * tokens_here) ** (-0.5)
    flat_shape = (tokens_here, head_count * HS)
    return (
        mixed.reshape(flat_shape),
        query_grad.reshape(flat_shape),
        key_grad.reshape(flat_shape),
        value_grad.reshape(flat_shape),
        owned_grad * factor,
        gain_sum * factor,
    )


def solution(mesh):
    placed = (
        P("seq", "fsdp"),
        P("seq", "fsdp"),
        P("seq", "fsdp"),
        P(None, "fsdp", "seq"),
        P("fsdp", None),
        P(),
        P("seq", "fsdp"),
    )
    seq_count, fsdp_count = mesh.devices.shape
    inner = 8 if seq_count % 8 == 0 else seq_count
    split = jax.sharding.Mesh(
        mesh.devices.reshape(seq_count // inner, inner, fsdp_count), (OUTER, INNER, "fsdp")
    )
    seq = (OUTER, INNER)

    def respec(spec):
        return P(*[seq if part == "seq" else part for part in spec])

    placed = tuple(respec(p) for p in placed)
    return jax.shard_map(
        local,
        mesh=split,
        in_specs=placed,
        out_specs=tuple(
            respec(p)
            for p in (
                P("seq", "fsdp"),
                P("seq", "fsdp"),
                P("seq", "fsdp"),
                P("seq", "fsdp"),
                P(None, "fsdp", "seq"),
                P("fsdp", None),
            )
        ),
        check_vma=False,
    )
```

```python
import jax
import jax.numpy as jnp
from jax import lax
from jax.sharding import PartitionSpec as P

HS = 128
BLK = 128


epsilon = 1.0
HIGH = lax.Precision.HIGHEST
OUTER = "seq_row"
INNER = "seq_col"


def shifted(x, dist, backward):
    count = lax.axis_size((OUTER, INNER))
    if backward:
        pairs = [(i, i - dist) for i in range(dist, count)]
    else:
        pairs = [(i, i + dist) for i in range(count - dist)]
    return lax.ppermute(x, (OUTER, INNER), pairs)


def masked_sum(mask, stacked):
    return jnp.sum(jnp.where(mask[:, None, None, None], stacked, 0.0), 0)


def carried_in(aggregate, last_open, backward):
    inner = lax.axis_size(INNER)
    outer = lax.axis_size(OUTER)
    col = lax.axis_index(INNER)
    row = lax.axis_index(OUTER)
    place = row * inner + col
    near = place + 1 if backward else place - 1
    bound = last_open(near)
    cols = jnp.arange(inner)
    rows = jnp.arange(outer)
    in_row = lax.all_gather(aggregate.astype(jnp.bfloat16), INNER).astype(jnp.float32)
    if backward:
        mine = (cols > col) & (row * inner + cols <= bound)
        row_bound = last_open(row * inner)
        carry = (row * inner + cols <= row_bound)
    else:
        mine = (cols < col) & (row * inner + cols >= bound)
        row_bound = last_open(row * inner + inner - 1)
        carry = (row * inner + cols >= row_bound)
    local_sum = masked_sum(mine, in_row)
    row_part = masked_sum(carry, in_row)
    across = lax.all_gather(row_part.astype(jnp.bfloat16), OUTER).astype(jnp.float32)
    bound_row = bound // inner
    if backward:
        take = (rows > row) & (rows <= bound_row)
    else:
        take = (rows < row) & (rows >= bound_row)
    far_sum = masked_sum(take, across)
    return local_sum + far_sum


def exchanged(x, bit):
    count = lax.axis_size((OUTER, INNER))
    return lax.ppermute(x, (OUTER, INNER), [(i, i ^ bit) for i in range(count)])


def gathered_columns(piece):
    count = lax.axis_size((OUTER, INNER))
    place = lax.axis_index((OUTER, INNER))
    bit = 1
    while bit < count:
        other = exchanged(piece, bit)
        upper = (place & bit) > 0
        piece = jnp.where(
            upper, jnp.concatenate([other, piece], -1), jnp.concatenate([piece, other], -1)
        )
        bit *= 2
    return piece


def summed_columns(part, extra):
    count = lax.axis_size((OUTER, INNER))
    place = lax.axis_index((OUTER, INNER))
    bit = count // 2
    while bit >= 1:
        half = part.shape[-1] // 2
        low, high = part[..., :half], part[..., half:]
        upper = (place & bit) > 0
        kept = jnp.where(upper, high, low)
        sent = jnp.where(upper, low, high)
        got = exchanged(jnp.concatenate([sent, extra[..., None]], -1), bit)
        part = kept + got[..., :half]
        extra = extra + got[..., half]
        bit //= 2
    return part, extra


def project(rows, weight):
    return jnp.einsum("bthd,hde->bthe", rows, weight, preferred_element_type=jnp.float32).astype(
        jnp.bfloat16
    )


def local(queries, keys, values, feature_weight, norm_gain, doc_bounds, out_grad):
    head_groups = lax.all_to_all(feature_weight, "fsdp", split_axis=0, concat_axis=1, tiled=True)
    weight_local = gathered_columns(head_groups)
    head_count = weight_local.shape[0]
    tokens_here = queries.shape[0]
    block_count = tokens_here // BLK
    block_shape = (block_count, BLK, head_count, HS)
    query_blocks = queries.reshape(block_shape)
    key_blocks = keys.reshape(block_shape)
    value_blocks = values.reshape(block_shape)

    place = lax.axis_index((OUTER, INNER))
    starts = doc_bounds[:, 0]
    start_device = starts // block_count

    def last_open(device):
        return jnp.max(jnp.where(start_device <= device, start_device, 0))

    def next_open(device):
        count = lax.axis_size((OUTER, INNER))
        return jnp.min(jnp.where(start_device >= device, start_device, count - 1))

    block_ids = place * block_count + jnp.arange(block_count, dtype=jnp.int32)
    starts_here = jnp.any(starts[None, :] == block_ids[:, None], axis=1)
    opened = jnp.cumsum(starts_here.astype(jnp.int32))
    reach_left = opened == 0
    reach_right = opened[-1] - opened == 0

    raw_updates = jnp.einsum(
        "bthd,bthf->bhdf", key_blocks, value_blocks, preferred_element_type=jnp.float32
    )
    zero_state = jnp.zeros(raw_updates.shape[1:], jnp.float32)
    running = zero_state
    prefix_list = []
    for position in range(block_count):
        held = jnp.where(starts_here[position], zero_state, running)
        prefix_list.append(held)
        running = held + raw_updates[position]
    entering = carried_in(running, last_open, False)
    raw_states = jnp.stack(prefix_list) + jnp.where(
        reach_left[:, None, None, None], entering[None], 0.0
    )

    qfeat = project(query_blocks, weight_local)
    kfeat = project(key_blocks, weight_local)
    weight_f = weight_local.astype(jnp.float32)
    states = jnp.einsum("hde,bhdf->bhef", weight_f, raw_states, precision=HIGH)
    state_half = states.astype(jnp.bfloat16)
    causal = jnp.arange(BLK)[:, None] >= jnp.arange(BLK)[None, :]
    scores = jnp.einsum("bthe,bshe->bhts", qfeat, kfeat, preferred_element_type=jnp.float32)
    prob_half = jnp.where(causal, scores, 0.0).astype(jnp.bfloat16)
    mixed_f = jnp.einsum("bthe,bhef->bthf", qfeat, state_half, preferred_element_type=jnp.float32)
    mixed_f = mixed_f + jnp.einsum(
        "bhts,bshf->bthf", prob_half, value_blocks, preferred_element_type=jnp.float32
    )
    gains = norm_gain.astype(jnp.float32)
    inverse = lax.rsqrt(jnp.mean(mixed_f * mixed_f, axis=-1, keepdims=True) + epsilon)
    mixed = (mixed_f * inverse * gains).astype(jnp.bfloat16)
    grad_y = out_grad.reshape(block_shape).astype(jnp.float32)
    scaled = grad_y * gains
    grad_mix = inverse * (
        scaled - mixed_f * inverse * inverse * jnp.mean(scaled * mixed_f, axis=-1, keepdims=True)
    )
    grad_half = grad_mix.astype(jnp.bfloat16)
    gain_part = jnp.sum(grad_y * mixed_f * inverse, axis=(0, 1))

    state_grads = jnp.einsum(
        "bthe,bthf->bhef", qfeat, grad_half, preferred_element_type=jnp.float32
    )
    dot_grads = jnp.einsum(
        "bthf,bshf->bhts", grad_half, value_blocks, preferred_element_type=jnp.float32
    )
    dot_half = jnp.where(causal, dot_grads, 0.0).astype(jnp.bfloat16)
    qfeat_grad = jnp.einsum(
        "bthf,bhef->bthe", grad_half, state_half, preferred_element_type=jnp.float32
    )
    qfeat_grad = (
        qfeat_grad
        + jnp.einsum("bhts,bshe->bthe", dot_half, kfeat, preferred_element_type=jnp.float32)
    ).astype(jnp.bfloat16)
    kfeat_inner = jnp.einsum(
        "bhts,bthe->bshe", dot_half, qfeat, preferred_element_type=jnp.float32
    )
    weight_part = jnp.einsum(
        "bthd,bthe->hde", query_blocks, qfeat_grad, preferred_element_type=jnp.float32
    )
    weight_part = weight_part + jnp.einsum(
        "bthd,bthe->hde", key_blocks, kfeat_inner.astype(jnp.bfloat16),
        preferred_element_type=jnp.float32,
    )
    weight_part = weight_part + jnp.einsum(
        "bhdf,bhef->hde", raw_states, state_grads, precision=HIGH
    )
    weight_columns, gain_sum = summed_columns(weight_part, gain_part)
    owned_grad = lax.all_to_all(weight_columns, "fsdp", split_axis=1, concat_axis=0, tiled=True)

    running = zero_state
    suffix_list = [zero_state] * block_count
    for position in reversed(range(block_count)):
        suffix_list[position] = running
        running = jnp.where(starts_here[position], zero_state, running + state_grads[position])
    leaving = carried_in(running, next_open, True)
    suffix = jnp.stack(suffix_list) + jnp.where(
        reach_right[:, None, None, None], leaving[None], 0.0
    )
    suffix_half = suffix.astype(jnp.bfloat16)
    kfeat_grad = jnp.einsum(
        "bshf,bhef->bshe", value_blocks, suffix_half, preferred_element_type=jnp.float32
    )
    kfeat_grad = (kfeat_grad + kfeat_inner).astype(jnp.bfloat16)
    value_grad = jnp.einsum(
        "bshe,bhef->bshf", kfeat, suffix_half, preferred_element_type=jnp.float32
    )
    value_grad = (
        value_grad
        + jnp.einsum("bhts,bthf->bshf", prob_half, grad_half, preferred_element_type=jnp.float32)
    ).astype(jnp.bfloat16)
    query_grad = jnp.einsum(
        "bthe,hde->bthd", qfeat_grad, weight_local, preferred_element_type=jnp.float32
    ).astype(jnp.bfloat16)
    key_grad = jnp.einsum(
        "bthe,hde->bthd", kfeat_grad, weight_local, preferred_element_type=jnp.float32
    ).astype(jnp.bfloat16)
    factor = (lax.axis_size((OUTER, INNER)) * tokens_here) ** (-0.5)
    flat_shape = (tokens_here, head_count * HS)
    return (
        mixed.reshape(flat_shape),
        query_grad.reshape(flat_shape),
        key_grad.reshape(flat_shape),
        value_grad.reshape(flat_shape),
        owned_grad * factor,
        gain_sum * factor,
    )


def solution(mesh):
    placed = (
        P("seq", "fsdp"),
        P("seq", "fsdp"),
        P("seq", "fsdp"),
        P(None, "fsdp", "seq"),
        P("fsdp", None),
        P(),
        P("seq", "fsdp"),
    )
    seq_count, fsdp_count = mesh.devices.shape
    inner = 8 if seq_count % 8 == 0 else seq_count
    split = jax.sharding.Mesh(
        mesh.devices.reshape(seq_count // inner, inner, fsdp_count), (OUTER, INNER, "fsdp")
    )
    seq = (OUTER, INNER)

    def respec(spec):
        return P(*[seq if part == "seq" else part for part in spec])

    placed = tuple(respec(p) for p in placed)
    return jax.shard_map(
        local,
        mesh=split,
        in_specs=placed,
        out_specs=tuple(
            respec(p)
            for p in (
                P("seq", "fsdp"),
                P("seq", "fsdp"),
                P("seq", "fsdp"),
                P("seq", "fsdp"),
                P(None, "fsdp", "seq"),
                P("fsdp", None),
            )
        ),
        check_vma=False,
    )
```

```python
import jax
import jax.numpy as jnp
from jax import lax
from jax.sharding import PartitionSpec as P

HS = 128
BLK = 128


epsilon = 1.0
HIGH = lax.Precision.HIGHEST
OUTER = "seq_row"
INNER = "seq_col"


def shifted(x, dist, backward):
    count = lax.axis_size((OUTER, INNER))
    if backward:
        pairs = [(i, i - dist) for i in range(dist, count)]
    else:
        pairs = [(i, i + dist) for i in range(count - dist)]
    return lax.ppermute(x, (OUTER, INNER), pairs)


def masked_sum(mask, stacked):
    return jnp.sum(jnp.where(mask[:, None, None, None], stacked, 0.0), 0)


def carried_in(aggregate, last_open, backward, kind, extra=None):
    inner = lax.axis_size(INNER)
    outer = lax.axis_size(OUTER)
    col = lax.axis_index(INNER)
    row = lax.axis_index(OUTER)
    place = row * inner + col
    near = place + 1 if backward else place - 1
    bound = last_open(near)
    cols = jnp.arange(inner)
    rows = jnp.arange(outer)
    width = aggregate.shape[-1]
    sent = aggregate.astype(kind)
    if extra is not None:
        sent = jnp.concatenate([sent, extra.astype(kind)], -1)
    in_row = lax.all_gather(sent, INNER)
    if extra is not None:
        row_extra = jnp.moveaxis(in_row[..., width:], 0, -2)
        row_extra = row_extra.reshape(row_extra.shape[:-2] + (-1,))
    in_row = in_row[..., :width].astype(jnp.float32)
    if backward:
        mine = (cols > col) & (row * inner + cols <= bound)
        row_bound = last_open(row * inner)
        carry = (row * inner + cols <= row_bound)
    else:
        mine = (cols < col) & (row * inner + cols >= bound)
        row_bound = last_open(row * inner + inner - 1)
        carry = (row * inner + cols >= row_bound)
    local_sum = masked_sum(mine, in_row)
    row_part = masked_sum(carry, in_row)
    sent = row_part.astype(kind)
    if extra is not None:
        sent = jnp.concatenate([sent, row_extra.astype(kind)], -1)
    across = lax.all_gather(sent, OUTER)
    if extra is not None:
        all_extra = jnp.moveaxis(across[..., width:], 0, -2)
        all_extra = all_extra.reshape(all_extra.shape[:-2] + (-1,))
    across = across[..., :width].astype(jnp.float32)
    bound_row = bound // inner
    if backward:
        take = (rows > row) & (rows <= bound_row)
    else:
        take = (rows < row) & (rows >= bound_row)
    far_sum = masked_sum(take, across)
    if extra is not None:
        return local_sum + far_sum, all_extra
    return local_sum + far_sum


def exchanged(x, bit):
    count = lax.axis_size((OUTER, INNER))
    return lax.ppermute(x, (OUTER, INNER), [(i, i ^ bit) for i in range(count)])


def gathered_columns(piece):
    count = lax.axis_size((OUTER, INNER))
    place = lax.axis_index((OUTER, INNER))
    bit = 1
    while bit < count:
        other = exchanged(piece, bit)
        upper = (place & bit) > 0
        piece = jnp.where(
            upper, jnp.concatenate([other, piece], -1), jnp.concatenate([piece, other], -1)
        )
        bit *= 2
    return piece


def summed_columns(part, extra):
    count = lax.axis_size((OUTER, INNER))
    place = lax.axis_index((OUTER, INNER))
    bit = count // 2
    while bit >= 1:
        half = part.shape[-1] // 2
        low, high = part[..., :half], part[..., half:]
        upper = (place & bit) > 0
        kept = jnp.where(upper, high, low)
        sent = jnp.where(upper, low, high)
        got = exchanged(jnp.concatenate([sent, extra[..., None]], -1), bit)
        part = kept + got[..., :half]
        extra = extra + got[..., half]
        bit //= 2
    return part, extra


def project(rows, weight):
    return jnp.einsum("bthd,hde->bthe", rows, weight, preferred_element_type=jnp.float32).astype(
        jnp.bfloat16
    )


def local(queries, keys, values, feature_weight, norm_gain, doc_bounds, out_grad):
    head_groups = lax.all_to_all(feature_weight, "fsdp", split_axis=0, concat_axis=1, tiled=True)
    head_count = head_groups.shape[0]
    tokens_here = queries.shape[0]
    block_count = tokens_here // BLK
    block_shape = (block_count, BLK, head_count, HS)
    query_blocks = queries.reshape(block_shape)
    key_blocks = keys.reshape(block_shape)
    value_blocks = values.reshape(block_shape)

    place = lax.axis_index((OUTER, INNER))
    starts = doc_bounds[:, 0]
    start_device = starts // block_count

    def last_open(device):
        return jnp.max(jnp.where(start_device <= device, start_device, 0))

    def next_open(device):
        count = lax.axis_size((OUTER, INNER))
        return jnp.min(jnp.where(start_device >= device, start_device, count - 1))

    block_ids = place * block_count + jnp.arange(block_count, dtype=jnp.int32)
    starts_here = jnp.any(starts[None, :] == block_ids[:, None], axis=1)
    opened = jnp.cumsum(starts_here.astype(jnp.int32))
    reach_left = opened == 0
    reach_right = opened[-1] - opened == 0

    raw_updates = jnp.einsum(
        "bthd,bthf->bhdf", key_blocks, value_blocks, preferred_element_type=jnp.float32
    )
    zero_state = jnp.zeros(raw_updates.shape[1:], jnp.float32)
    running = zero_state
    prefix_list = []
    for position in range(block_count):
        held = jnp.where(starts_here[position], zero_state, running)
        prefix_list.append(held)
        running = held + raw_updates[position]
    entering, weight_local = carried_in(
        running, last_open, False, jnp.bfloat16, extra=head_groups
    )
    raw_states = jnp.stack(prefix_list) + jnp.where(
        reach_left[:, None, None, None], entering[None], 0.0
    )

    qfeat = project(query_blocks, weight_local)
    kfeat = project(key_blocks, weight_local)
    weight_f = weight_local.astype(jnp.float32)
    states = jnp.einsum("hde,bhdf->bhef", weight_f, raw_states, precision=HIGH)
    state_half = states.astype(jnp.bfloat16)
    causal = jnp.arange(BLK)[:, None] >= jnp.arange(BLK)[None, :]
    scores = jnp.einsum("bthe,bshe->bhts", qfeat, kfeat, preferred_element_type=jnp.float32)
    prob_half = jnp.where(causal, scores, 0.0).astype(jnp.bfloat16)
    mixed_f = jnp.einsum("bthe,bhef->bthf", qfeat, state_half, preferred_element_type=jnp.float32)
    mixed_f = mixed_f + jnp.einsum(
        "bhts,bshf->bthf", prob_half, value_blocks, preferred_element_type=jnp.float32
    )
    gains = norm_gain.astype(jnp.float32)
    inverse = lax.rsqrt(jnp.mean(mixed_f * mixed_f, axis=-1, keepdims=True) + epsilon)
    mixed = (mixed_f * inverse * gains).astype(jnp.bfloat16)
    grad_y = out_grad.reshape(block_shape).astype(jnp.float32)
    scaled = grad_y * gains
    grad_mix = inverse * (
        scaled - mixed_f * inverse * inverse * jnp.mean(scaled * mixed_f, axis=-1, keepdims=True)
    )
    grad_half = grad_mix.astype(jnp.bfloat16)
    gain_part = jnp.sum(grad_y * mixed_f * inverse, axis=(0, 1))

    state_grads = jnp.einsum(
        "bthe,bthf->bhef", qfeat, grad_half, preferred_element_type=jnp.float32
    )
    dot_grads = jnp.einsum(
        "bthf,bshf->bhts", grad_half, value_blocks, preferred_element_type=jnp.float32
    )
    dot_half = jnp.where(causal, dot_grads, 0.0).astype(jnp.bfloat16)
    qfeat_grad = jnp.einsum(
        "bthf,bhef->bthe", grad_half, state_half, preferred_element_type=jnp.float32
    )
    qfeat_grad = (
        qfeat_grad
        + jnp.einsum("bhts,bshe->bthe", dot_half, kfeat, preferred_element_type=jnp.float32)
    ).astype(jnp.bfloat16)
    kfeat_inner = jnp.einsum(
        "bhts,bthe->bshe", dot_half, qfeat, preferred_element_type=jnp.float32
    )
    weight_part = jnp.einsum(
        "bthd,bthe->hde", query_blocks, qfeat_grad, preferred_element_type=jnp.float32
    )
    weight_part = weight_part + jnp.einsum(
        "bthd,bthe->hde", key_blocks, kfeat_inner.astype(jnp.bfloat16),
        preferred_element_type=jnp.float32,
    )
    weight_part = weight_part + jnp.einsum(
        "bhdf,bhef->hde", raw_states, state_grads, precision=HIGH
    )
    weight_columns, gain_sum = summed_columns(weight_part, gain_part)
    owned_grad = lax.all_to_all(weight_columns, "fsdp", split_axis=1, concat_axis=0, tiled=True)

    running = zero_state
    suffix_list = [zero_state] * block_count
    for position in reversed(range(block_count)):
        suffix_list[position] = running
        running = jnp.where(starts_here[position], zero_state, running + state_grads[position])
    leaving = carried_in(running, next_open, True, jnp.float32)
    suffix = jnp.stack(suffix_list) + jnp.where(
        reach_right[:, None, None, None], leaving[None], 0.0
    )
    suffix_half = suffix.astype(jnp.bfloat16)
    kfeat_grad = jnp.einsum(
        "bshf,bhef->bshe", value_blocks, suffix_half, preferred_element_type=jnp.float32
    )
    kfeat_grad = (kfeat_grad + kfeat_inner).astype(jnp.bfloat16)
    value_grad = jnp.einsum(
        "bshe,bhef->bshf", kfeat, suffix_half, preferred_element_type=jnp.float32
    )
    value_grad = (
        value_grad
        + jnp.einsum("bhts,bthf->bshf", prob_half, grad_half, preferred_element_type=jnp.float32)
    ).astype(jnp.bfloat16)
    query_grad = jnp.einsum(
        "bthe,hde->bthd", qfeat_grad, weight_local, preferred_element_type=jnp.float32
    ).astype(jnp.bfloat16)
    key_grad = jnp.einsum(
        "bthe,hde->bthd", kfeat_grad, weight_local, preferred_element_type=jnp.float32
    ).astype(jnp.bfloat16)
    factor = (lax.axis_size((OUTER, INNER)) * tokens_here) ** (-0.5)
    flat_shape = (tokens_here, head_count * HS)
    return (
        mixed.reshape(flat_shape),
        query_grad.reshape(flat_shape),
        key_grad.reshape(flat_shape),
        value_grad.reshape(flat_shape),
        owned_grad * factor,
        gain_sum * factor,
    )


def solution(mesh):
    placed = (
        P("seq", "fsdp"),
        P("seq", "fsdp"),
        P("seq", "fsdp"),
        P(None, "fsdp", "seq"),
        P("fsdp", None),
        P(),
        P("seq", "fsdp"),
    )
    seq_count, fsdp_count = mesh.devices.shape
    inner = 8 if seq_count % 8 == 0 else seq_count
    split = jax.sharding.Mesh(
        mesh.devices.reshape(seq_count // inner, inner, fsdp_count), (OUTER, INNER, "fsdp")
    )
    seq = (OUTER, INNER)

    def respec(spec):
        return P(*[seq if part == "seq" else part for part in spec])

    placed = tuple(respec(p) for p in placed)
    return jax.shard_map(
        local,
        mesh=split,
        in_specs=placed,
        out_specs=tuple(
            respec(p)
            for p in (
                P("seq", "fsdp"),
                P("seq", "fsdp"),
                P("seq", "fsdp"),
                P("seq", "fsdp"),
                P(None, "fsdp", "seq"),
                P("fsdp", None),
            )
        ),
        check_vma=False,
    )
```

```python
import jax
import jax.numpy as jnp
from jax import lax
from jax.sharding import PartitionSpec as P

HS = 128
BLK = 128


epsilon = 1.0
HIGH = lax.Precision.HIGHEST
OUTER = "seq_row"
INNER = "seq_col"


def shifted(x, dist, backward):
    count = lax.axis_size((OUTER, INNER))
    if backward:
        pairs = [(i, i - dist) for i in range(dist, count)]
    else:
        pairs = [(i, i + dist) for i in range(count - dist)]
    return lax.ppermute(x, (OUTER, INNER), pairs)


def masked_sum(mask, stacked):
    return jnp.sum(jnp.where(mask[:, None, None, None], stacked, 0.0), 0)


def carried_in(aggregate, last_open, backward, kind, far_kind, extra=None):
    inner = lax.axis_size(INNER)
    outer = lax.axis_size(OUTER)
    col = lax.axis_index(INNER)
    row = lax.axis_index(OUTER)
    place = row * inner + col
    near = place + 1 if backward else place - 1
    bound = last_open(near)
    cols = jnp.arange(inner)
    rows = jnp.arange(outer)
    width = aggregate.shape[-1]
    sent = aggregate.astype(kind)
    if extra is not None:
        sent = jnp.concatenate([sent, extra.astype(kind)], -1)
    in_row = lax.all_gather(sent, INNER)
    if extra is not None:
        row_extra = jnp.moveaxis(in_row[..., width:], 0, -2)
        row_extra = row_extra.reshape(row_extra.shape[:-2] + (-1,))
    in_row = in_row[..., :width].astype(jnp.float32)
    if backward:
        mine = (cols > col) & (row * inner + cols <= bound)
        row_bound = last_open(row * inner)
        carry = (row * inner + cols <= row_bound)
    else:
        mine = (cols < col) & (row * inner + cols >= bound)
        row_bound = last_open(row * inner + inner - 1)
        carry = (row * inner + cols >= row_bound)
    local_sum = masked_sum(mine, in_row)
    row_part = masked_sum(carry, in_row)
    sent = row_part.astype(far_kind)
    if extra is not None:
        sent = jnp.concatenate([sent, row_extra.astype(far_kind)], -1)
    across = lax.all_gather(sent, OUTER)
    if extra is not None:
        all_extra = jnp.moveaxis(across[..., width:], 0, -2)
        all_extra = all_extra.reshape(all_extra.shape[:-2] + (-1,))
    across = across[..., :width].astype(jnp.float32)
    bound_row = bound // inner
    if backward:
        take = (rows > row) & (rows <= bound_row)
    else:
        take = (rows < row) & (rows >= bound_row)
    far_sum = masked_sum(take, across)
    if extra is not None:
        return local_sum + far_sum, all_extra
    return local_sum + far_sum


def exchanged(x, bit):
    count = lax.axis_size((OUTER, INNER))
    return lax.ppermute(x, (OUTER, INNER), [(i, i ^ bit) for i in range(count)])


def gathered_columns(piece):
    count = lax.axis_size((OUTER, INNER))
    place = lax.axis_index((OUTER, INNER))
    bit = 1
    while bit < count:
        other = exchanged(piece, bit)
        upper = (place & bit) > 0
        piece = jnp.where(
            upper, jnp.concatenate([other, piece], -1), jnp.concatenate([piece, other], -1)
        )
        bit *= 2
    return piece


def summed_columns(part, extra):
    count = lax.axis_size((OUTER, INNER))
    place = lax.axis_index((OUTER, INNER))
    bit = count // 2
    while bit >= 1:
        half = part.shape[-1] // 2
        low, high = part[..., :half], part[..., half:]
        upper = (place & bit) > 0
        kept = jnp.where(upper, high, low)
        sent = jnp.where(upper, low, high)
        got = exchanged(jnp.concatenate([sent, extra[..., None]], -1), bit)
        part = kept + got[..., :half]
        extra = extra + got[..., half]
        bit //= 2
    return part, extra


def project(rows, weight):
    return jnp.einsum("bthd,hde->bthe", rows, weight, preferred_element_type=jnp.float32).astype(
        jnp.bfloat16
    )


def local(queries, keys, values, feature_weight, norm_gain, doc_bounds, out_grad):
    head_groups = lax.all_to_all(feature_weight, "fsdp", split_axis=0, concat_axis=1, tiled=True)
    head_count = head_groups.shape[0]
    tokens_here = queries.shape[0]
    block_count = tokens_here // BLK
    block_shape = (block_count, BLK, head_count, HS)
    query_blocks = queries.reshape(block_shape)
    key_blocks = keys.reshape(block_shape)
    value_blocks = values.reshape(block_shape)

    place = lax.axis_index((OUTER, INNER))
    starts = doc_bounds[:, 0]
    start_device = starts // block_count

    def last_open(device):
        return jnp.max(jnp.where(start_device <= device, start_device, 0))

    def next_open(device):
        count = lax.axis_size((OUTER, INNER))
        return jnp.min(jnp.where(start_device >= device, start_device, count - 1))

    block_ids = place * block_count + jnp.arange(block_count, dtype=jnp.int32)
    starts_here = jnp.any(starts[None, :] == block_ids[:, None], axis=1)
    opened = jnp.cumsum(starts_here.astype(jnp.int32))
    reach_left = opened == 0
    reach_right = opened[-1] - opened == 0

    raw_updates = jnp.einsum(
        "bthd,bthf->bhdf", key_blocks, value_blocks, preferred_element_type=jnp.float32
    )
    zero_state = jnp.zeros(raw_updates.shape[1:], jnp.float32)
    running = zero_state
    prefix_list = []
    for position in range(block_count):
        held = jnp.where(starts_here[position], zero_state, running)
        prefix_list.append(held)
        running = held + raw_updates[position]
    entering, weight_local = carried_in(
        running, last_open, False, jnp.bfloat16, jnp.bfloat16, extra=head_groups
    )
    raw_states = jnp.stack(prefix_list) + jnp.where(
        reach_left[:, None, None, None], entering[None], 0.0
    )

    qfeat = project(query_blocks, weight_local)
    kfeat = project(key_blocks, weight_local)
    weight_f = weight_local.astype(jnp.float32)
    states = jnp.einsum("hde,bhdf->bhef", weight_f, raw_states, precision=HIGH)
    state_half = states.astype(jnp.bfloat16)
    causal = jnp.arange(BLK)[:, None] >= jnp.arange(BLK)[None, :]
    scores = jnp.einsum("bthe,bshe->bhts", qfeat, kfeat, preferred_element_type=jnp.float32)
    prob_half = jnp.where(causal, scores, 0.0).astype(jnp.bfloat16)
    mixed_f = jnp.einsum("bthe,bhef->bthf", qfeat, state_half, preferred_element_type=jnp.float32)
    mixed_f = mixed_f + jnp.einsum(
        "bhts,bshf->bthf", prob_half, value_blocks, preferred_element_type=jnp.float32
    )
    gains = norm_gain.astype(jnp.float32)
    inverse = lax.rsqrt(jnp.mean(mixed_f * mixed_f, axis=-1, keepdims=True) + epsilon)
    mixed = (mixed_f * inverse * gains).astype(jnp.bfloat16)
    grad_y = out_grad.reshape(block_shape).astype(jnp.float32)
    scaled = grad_y * gains
    grad_mix = inverse * (
        scaled - mixed_f * inverse * inverse * jnp.mean(scaled * mixed_f, axis=-1, keepdims=True)
    )
    grad_half = grad_mix.astype(jnp.bfloat16)
    gain_part = jnp.sum(grad_y * mixed_f * inverse, axis=(0, 1))

    state_grads = jnp.einsum(
        "bthe,bthf->bhef", qfeat, grad_half, preferred_element_type=jnp.float32
    )
    dot_grads = jnp.einsum(
        "bthf,bshf->bhts", grad_half, value_blocks, preferred_element_type=jnp.float32
    )
    dot_half = jnp.where(causal, dot_grads, 0.0).astype(jnp.bfloat16)
    qfeat_grad = jnp.einsum(
        "bthf,bhef->bthe", grad_half, state_half, preferred_element_type=jnp.float32
    )
    qfeat_grad = (
        qfeat_grad
        + jnp.einsum("bhts,bshe->bthe", dot_half, kfeat, preferred_element_type=jnp.float32)
    ).astype(jnp.bfloat16)
    kfeat_inner = jnp.einsum(
        "bhts,bthe->bshe", dot_half, qfeat, preferred_element_type=jnp.float32
    )
    weight_part = jnp.einsum(
        "bthd,bthe->hde", query_blocks, qfeat_grad, preferred_element_type=jnp.float32
    )
    weight_part = weight_part + jnp.einsum(
        "bthd,bthe->hde", key_blocks, kfeat_inner.astype(jnp.bfloat16),
        preferred_element_type=jnp.float32,
    )
    weight_part = weight_part + jnp.einsum(
        "bhdf,bhef->hde", raw_states, state_grads, precision=HIGH
    )
    weight_columns, gain_sum = summed_columns(weight_part, gain_part)
    owned_grad = lax.all_to_all(weight_columns, "fsdp", split_axis=1, concat_axis=0, tiled=True)

    running = zero_state
    suffix_list = [zero_state] * block_count
    for position in reversed(range(block_count)):
        suffix_list[position] = running
        running = jnp.where(starts_here[position], zero_state, running + state_grads[position])
    leaving = carried_in(running, next_open, True, jnp.bfloat16, jnp.float32)
    suffix = jnp.stack(suffix_list) + jnp.where(
        reach_right[:, None, None, None], leaving[None], 0.0
    )
    suffix_half = suffix.astype(jnp.bfloat16)
    kfeat_grad = jnp.einsum(
        "bshf,bhef->bshe", value_blocks, suffix_half, preferred_element_type=jnp.float32
    )
    kfeat_grad = (kfeat_grad + kfeat_inner).astype(jnp.bfloat16)
    value_grad = jnp.einsum(
        "bshe,bhef->bshf", kfeat, suffix_half, preferred_element_type=jnp.float32
    )
    value_grad = (
        value_grad
        + jnp.einsum("bhts,bthf->bshf", prob_half, grad_half, preferred_element_type=jnp.float32)
    ).astype(jnp.bfloat16)
    query_grad = jnp.einsum(
        "bthe,hde->bthd", qfeat_grad, weight_local, preferred_element_type=jnp.float32
    ).astype(jnp.bfloat16)
    key_grad = jnp.einsum(
        "bthe,hde->bthd", kfeat_grad, weight_local, preferred_element_type=jnp.float32
    ).astype(jnp.bfloat16)
    factor = (lax.axis_size((OUTER, INNER)) * tokens_here) ** (-0.5)
    flat_shape = (tokens_here, head_count * HS)
    return (
        mixed.reshape(flat_shape),
        query_grad.reshape(flat_shape),
        key_grad.reshape(flat_shape),
        value_grad.reshape(flat_shape),
        owned_grad * factor,
        gain_sum * factor,
    )


def solution(mesh):
    placed = (
        P("seq", "fsdp"),
        P("seq", "fsdp"),
        P("seq", "fsdp"),
        P(None, "fsdp", "seq"),
        P("fsdp", None),
        P(),
        P("seq", "fsdp"),
    )
    seq_count, fsdp_count = mesh.devices.shape
    inner = 8 if seq_count % 8 == 0 else seq_count
    split = jax.sharding.Mesh(
        mesh.devices.reshape(seq_count // inner, inner, fsdp_count), (OUTER, INNER, "fsdp")
    )
    seq = (OUTER, INNER)

    def respec(spec):
        return P(*[seq if part == "seq" else part for part in spec])

    placed = tuple(respec(p) for p in placed)
    return jax.shard_map(
        local,
        mesh=split,
        in_specs=placed,
        out_specs=tuple(
            respec(p)
            for p in (
                P("seq", "fsdp"),
                P("seq", "fsdp"),
                P("seq", "fsdp"),
                P("seq", "fsdp"),
                P(None, "fsdp", "seq"),
                P("fsdp", None),
            )
        ),
        check_vma=False,
    )
```

```python
import jax
import jax.numpy as jnp
from jax import lax
from jax.sharding import PartitionSpec as P

HS = 128
BLK = 128


epsilon = 1.0
HIGH = lax.Precision.HIGHEST
OUTER = "seq_row"
INNER = "seq_col"


def shifted(x, dist, backward):
    count = lax.axis_size((OUTER, INNER))
    if backward:
        pairs = [(i, i - dist) for i in range(dist, count)]
    else:
        pairs = [(i, i + dist) for i in range(count - dist)]
    return lax.ppermute(x, (OUTER, INNER), pairs)


def masked_sum(mask, stacked):
    return jnp.sum(jnp.where(mask[:, None, None, None], stacked, 0.0), 0)


def carried_in(aggregate, last_open, backward, kind, far_kind, extra=None, tied=None):
    inner = lax.axis_size(INNER)
    outer = lax.axis_size(OUTER)
    col = lax.axis_index(INNER)
    row = lax.axis_index(OUTER)
    place = row * inner + col
    near = place + 1 if backward else place - 1
    bound = last_open(near)
    cols = jnp.arange(inner)
    rows = jnp.arange(outer)
    width = aggregate.shape[-1]
    sent = aggregate.astype(kind)
    if extra is not None:
        sent = jnp.concatenate([sent, extra.astype(kind)], -1)
    in_row = lax.all_gather(sent, INNER)
    if extra is not None:
        row_extra = jnp.moveaxis(in_row[..., width:], 0, -2)
        row_extra = row_extra.reshape(row_extra.shape[:-2] + (-1,))
    in_row = in_row[..., :width].astype(jnp.float32)
    if backward:
        mine = (cols > col) & (row * inner + cols <= bound)
        row_bound = last_open(row * inner)
        carry = (row * inner + cols <= row_bound)
    else:
        mine = (cols < col) & (row * inner + cols >= bound)
        row_bound = last_open(row * inner + inner - 1)
        carry = (row * inner + cols >= row_bound)
    local_sum = masked_sum(mine, in_row)
    row_part = masked_sum(carry, in_row)
    sent = row_part.astype(far_kind)
    if tied is not None:
        sent, tied = lax.optimization_barrier((sent, tied))
    if extra is not None:
        sent = jnp.concatenate([sent, row_extra.astype(far_kind)], -1)
    across = lax.all_gather(sent, OUTER)
    if extra is not None:
        all_extra = jnp.moveaxis(across[..., width:], 0, -2)
        all_extra = all_extra.reshape(all_extra.shape[:-2] + (-1,))
    across = across[..., :width].astype(jnp.float32)
    bound_row = bound // inner
    if backward:
        take = (rows > row) & (rows <= bound_row)
    else:
        take = (rows < row) & (rows >= bound_row)
    far_sum = masked_sum(take, across)
    if extra is not None:
        return local_sum + far_sum, all_extra
    if tied is not None:
        return local_sum + far_sum, tied
    return local_sum + far_sum


def exchanged(x, bit):
    count = lax.axis_size((OUTER, INNER))
    return lax.ppermute(x, (OUTER, INNER), [(i, i ^ bit) for i in range(count)])


def gathered_columns(piece):
    count = lax.axis_size((OUTER, INNER))
    place = lax.axis_index((OUTER, INNER))
    bit = 1
    while bit < count:
        other = exchanged(piece, bit)
        upper = (place & bit) > 0
        piece = jnp.where(
            upper, jnp.concatenate([other, piece], -1), jnp.concatenate([piece, other], -1)
        )
        bit *= 2
    return piece


def summed_columns(part, extra):
    count = lax.axis_size((OUTER, INNER))
    place = lax.axis_index((OUTER, INNER))
    bit = count // 2
    while bit >= 1:
        half = part.shape[-1] // 2
        low, high = part[..., :half], part[..., half:]
        upper = (place & bit) > 0
        kept = jnp.where(upper, high, low)
        sent = jnp.where(upper, low, high)
        got = exchanged(jnp.concatenate([sent, extra[..., None]], -1), bit)
        part = kept + got[..., :half]
        extra = extra + got[..., half]
        bit //= 2
    return part, extra


def project(rows, weight):
    return jnp.einsum("bthd,hde->bthe", rows, weight, preferred_element_type=jnp.float32).astype(
        jnp.bfloat16
    )


def local(queries, keys, values, feature_weight, norm_gain, doc_bounds, out_grad):
    head_groups = lax.all_to_all(feature_weight, "fsdp", split_axis=0, concat_axis=1, tiled=True)
    head_count = head_groups.shape[0]
    tokens_here = queries.shape[0]
    block_count = tokens_here // BLK
    block_shape = (block_count, BLK, head_count, HS)
    query_blocks = queries.reshape(block_shape)
    key_blocks = keys.reshape(block_shape)
    value_blocks = values.reshape(block_shape)

    place = lax.axis_index((OUTER, INNER))
    starts = doc_bounds[:, 0]
    start_device = starts // block_count

    def last_open(device):
        return jnp.max(jnp.where(start_device <= device, start_device, 0))

    def next_open(device):
        count = lax.axis_size((OUTER, INNER))
        return jnp.min(jnp.where(start_device >= device, start_device, count - 1))

    block_ids = place * block_count + jnp.arange(block_count, dtype=jnp.int32)
    starts_here = jnp.any(starts[None, :] == block_ids[:, None], axis=1)
    opened = jnp.cumsum(starts_here.astype(jnp.int32))
    reach_left = opened == 0
    reach_right = opened[-1] - opened == 0

    raw_updates = jnp.einsum(
        "bthd,bthf->bhdf", key_blocks, value_blocks, preferred_element_type=jnp.float32
    )
    zero_state = jnp.zeros(raw_updates.shape[1:], jnp.float32)
    running = zero_state
    prefix_list = []
    for position in range(block_count):
        held = jnp.where(starts_here[position], zero_state, running)
        prefix_list.append(held)
        running = held + raw_updates[position]
    entering, weight_local = carried_in(
        running, last_open, False, jnp.bfloat16, jnp.bfloat16, extra=head_groups
    )
    raw_states = jnp.stack(prefix_list) + jnp.where(
        reach_left[:, None, None, None], entering[None], 0.0
    )

    qfeat = project(query_blocks, weight_local)
    kfeat = project(key_blocks, weight_local)
    weight_f = weight_local.astype(jnp.float32)
    states = jnp.einsum("hde,bhdf->bhef", weight_f, raw_states, precision=HIGH)
    state_half = states.astype(jnp.bfloat16)
    causal = jnp.arange(BLK)[:, None] >= jnp.arange(BLK)[None, :]
    scores = jnp.einsum("bthe,bshe->bhts", qfeat, kfeat, preferred_element_type=jnp.float32)
    prob_half = jnp.where(causal, scores, 0.0).astype(jnp.bfloat16)
    mixed_f = jnp.einsum("bthe,bhef->bthf", qfeat, state_half, preferred_element_type=jnp.float32)
    mixed_f = mixed_f + jnp.einsum(
        "bhts,bshf->bthf", prob_half, value_blocks, preferred_element_type=jnp.float32
    )
    gains = norm_gain.astype(jnp.float32)
    inverse = lax.rsqrt(jnp.mean(mixed_f * mixed_f, axis=-1, keepdims=True) + epsilon)
    mixed = (mixed_f * inverse * gains).astype(jnp.bfloat16)
    grad_y = out_grad.reshape(block_shape).astype(jnp.float32)
    scaled = grad_y * gains
    grad_mix = inverse * (
        scaled - mixed_f * inverse * inverse * jnp.mean(scaled * mixed_f, axis=-1, keepdims=True)
    )
    grad_half = grad_mix.astype(jnp.bfloat16)
    gain_part = jnp.sum(grad_y * mixed_f * inverse, axis=(0, 1))

    state_grads = jnp.einsum(
        "bthe,bthf->bhef", qfeat, grad_half, preferred_element_type=jnp.float32
    )
    dot_grads = jnp.einsum(
        "bthf,bshf->bhts", grad_half, value_blocks, preferred_element_type=jnp.float32
    )
    dot_half = jnp.where(causal, dot_grads, 0.0).astype(jnp.bfloat16)
    qfeat_grad = jnp.einsum(
        "bthf,bhef->bthe", grad_half, state_half, preferred_element_type=jnp.float32
    )
    qfeat_grad = (
        qfeat_grad
        + jnp.einsum("bhts,bshe->bthe", dot_half, kfeat, preferred_element_type=jnp.float32)
    ).astype(jnp.bfloat16)
    kfeat_inner = jnp.einsum(
        "bhts,bthe->bshe", dot_half, qfeat, preferred_element_type=jnp.float32
    )
    weight_part = jnp.einsum(
        "bthd,bthe->hde", query_blocks, qfeat_grad, preferred_element_type=jnp.float32
    )
    weight_part = weight_part + jnp.einsum(
        "bthd,bthe->hde", key_blocks, kfeat_inner.astype(jnp.bfloat16),
        preferred_element_type=jnp.float32,
    )
    weight_part = weight_part + jnp.einsum(
        "bhdf,bhef->hde", raw_states, state_grads, precision=HIGH
    )

    running = zero_state
    suffix_list = [zero_state] * block_count
    for position in reversed(range(block_count)):
        suffix_list[position] = running
        running = jnp.where(starts_here[position], zero_state, running + state_grads[position])
    leaving, (weight_part, gain_part) = carried_in(
        running, next_open, True, jnp.bfloat16, jnp.float32, tied=(weight_part, gain_part)
    )
    weight_columns, gain_sum = summed_columns(weight_part, gain_part)
    owned_grad = lax.all_to_all(weight_columns, "fsdp", split_axis=1, concat_axis=0, tiled=True)
    suffix = jnp.stack(suffix_list) + jnp.where(
        reach_right[:, None, None, None], leaving[None], 0.0
    )
    suffix_half = suffix.astype(jnp.bfloat16)
    kfeat_grad = jnp.einsum(
        "bshf,bhef->bshe", value_blocks, suffix_half, preferred_element_type=jnp.float32
    )
    kfeat_grad = (kfeat_grad + kfeat_inner).astype(jnp.bfloat16)
    value_grad = jnp.einsum(
        "bshe,bhef->bshf", kfeat, suffix_half, preferred_element_type=jnp.float32
    )
    value_grad = (
        value_grad
        + jnp.einsum("bhts,bthf->bshf", prob_half, grad_half, preferred_element_type=jnp.float32)
    ).astype(jnp.bfloat16)
    query_grad = jnp.einsum(
        "bthe,hde->bthd", qfeat_grad, weight_local, preferred_element_type=jnp.float32
    ).astype(jnp.bfloat16)
    key_grad = jnp.einsum(
        "bthe,hde->bthd", kfeat_grad, weight_local, preferred_element_type=jnp.float32
    ).astype(jnp.bfloat16)
    factor = (lax.axis_size((OUTER, INNER)) * tokens_here) ** (-0.5)
    flat_shape = (tokens_here, head_count * HS)
    return (
        mixed.reshape(flat_shape),
        query_grad.reshape(flat_shape),
        key_grad.reshape(flat_shape),
        value_grad.reshape(flat_shape),
        owned_grad * factor,
        gain_sum * factor,
    )


def solution(mesh):
    placed = (
        P("seq", "fsdp"),
        P("seq", "fsdp"),
        P("seq", "fsdp"),
        P(None, "fsdp", "seq"),
        P("fsdp", None),
        P(),
        P("seq", "fsdp"),
    )
    seq_count, fsdp_count = mesh.devices.shape
    inner = 8 if seq_count % 8 == 0 else seq_count
    split = jax.sharding.Mesh(
        mesh.devices.reshape(seq_count // inner, inner, fsdp_count), (OUTER, INNER, "fsdp")
    )
    seq = (OUTER, INNER)

    def respec(spec):
        return P(*[seq if part == "seq" else part for part in spec])

    placed = tuple(respec(p) for p in placed)
    return jax.shard_map(
        local,
        mesh=split,
        in_specs=placed,
        out_specs=tuple(
            respec(p)
            for p in (
                P("seq", "fsdp"),
                P("seq", "fsdp"),
                P("seq", "fsdp"),
                P("seq", "fsdp"),
                P(None, "fsdp", "seq"),
                P("fsdp", None),
            )
        ),
        check_vma=False,
    )
```

```python
import jax
import jax.numpy as jnp
from jax import lax
from jax.sharding import PartitionSpec as P

HS = 128
BLK = 128


epsilon = 1.0
HIGH = lax.Precision.HIGHEST
OUTER = "seq_row"
INNER = "seq_col"


def shifted(x, dist, backward):
    count = lax.axis_size((OUTER, INNER))
    if backward:
        pairs = [(i, i - dist) for i in range(dist, count)]
    else:
        pairs = [(i, i + dist) for i in range(count - dist)]
    return lax.ppermute(x, (OUTER, INNER), pairs)


def masked_sum(mask, stacked):
    return jnp.sum(jnp.where(mask[:, None, None, None], stacked, 0.0), 0)


def carried_in(aggregate, last_open, backward, kind, far_kind, extra=None, tied=None):
    inner = lax.axis_size(INNER)
    outer = lax.axis_size(OUTER)
    col = lax.axis_index(INNER)
    row = lax.axis_index(OUTER)
    place = row * inner + col
    near = place + 1 if backward else place - 1
    bound = last_open(near)
    cols = jnp.arange(inner)
    rows = jnp.arange(outer)
    width = aggregate.shape[-1]
    sent = aggregate.astype(kind)
    if extra is not None:
        sent = jnp.concatenate([sent, extra.astype(kind)], -1)
    in_row = lax.all_gather(sent, INNER)
    if extra is not None:
        row_extra = jnp.moveaxis(in_row[..., width:], 0, -2)
        row_extra = row_extra.reshape(row_extra.shape[:-2] + (-1,))
    in_row = in_row[..., :width].astype(jnp.float32)
    if backward:
        mine = (cols > col) & (row * inner + cols <= bound)
        row_bound = last_open(row * inner)
        carry = (row * inner + cols <= row_bound)
    else:
        mine = (cols < col) & (row * inner + cols >= bound)
        row_bound = last_open(row * inner + inner - 1)
        carry = (row * inner + cols >= row_bound)
    local_sum = masked_sum(mine, in_row)
    row_part = masked_sum(carry, in_row)
    sent = row_part.astype(far_kind)
    if tied is not None:
        sent, tied = lax.optimization_barrier((sent, tied))
    if extra is not None:
        sent = jnp.concatenate([sent, row_extra.astype(far_kind)], -1)
    across = lax.all_gather(sent, OUTER)
    if extra is not None:
        all_extra = jnp.moveaxis(across[..., width:], 0, -2)
        all_extra = all_extra.reshape(all_extra.shape[:-2] + (-1,))
    across = across[..., :width].astype(jnp.float32)
    bound_row = bound // inner
    if backward:
        take = (rows > row) & (rows <= bound_row)
    else:
        take = (rows < row) & (rows >= bound_row)
    far_sum = masked_sum(take, across)
    if extra is not None:
        return local_sum + far_sum, all_extra
    if tied is not None:
        return local_sum + far_sum, tied
    return local_sum + far_sum


def exchanged(x, bit):
    count = lax.axis_size((OUTER, INNER))
    return lax.ppermute(x, (OUTER, INNER), [(i, i ^ bit) for i in range(count)])


def gathered_columns(piece):
    count = lax.axis_size((OUTER, INNER))
    place = lax.axis_index((OUTER, INNER))
    bit = 1
    while bit < count:
        other = exchanged(piece, bit)
        upper = (place & bit) > 0
        piece = jnp.where(
            upper, jnp.concatenate([other, piece], -1), jnp.concatenate([piece, other], -1)
        )
        bit *= 2
    return piece


def summed_columns(part, extra, first=None, last=1):
    count = lax.axis_size((OUTER, INNER))
    place = lax.axis_index((OUTER, INNER))
    bit = count // 2 if first is None else first
    while bit >= last:
        half = part.shape[-1] // 2
        low, high = part[..., :half], part[..., half:]
        upper = (place & bit) > 0
        kept = jnp.where(upper, high, low)
        sent = jnp.where(upper, low, high)
        got = exchanged(jnp.concatenate([sent, extra[..., None]], -1), bit)
        part = kept + got[..., :half]
        extra = extra + got[..., half]
        bit //= 2
    return part, extra


def project(rows, weight):
    return jnp.einsum("bthd,hde->bthe", rows, weight, preferred_element_type=jnp.float32).astype(
        jnp.bfloat16
    )


def local(queries, keys, values, feature_weight, norm_gain, doc_bounds, out_grad):
    head_groups = lax.all_to_all(feature_weight, "fsdp", split_axis=0, concat_axis=1, tiled=True)
    head_count = head_groups.shape[0]
    tokens_here = queries.shape[0]
    block_count = tokens_here // BLK
    block_shape = (block_count, BLK, head_count, HS)
    query_blocks = queries.reshape(block_shape)
    key_blocks = keys.reshape(block_shape)
    value_blocks = values.reshape(block_shape)

    place = lax.axis_index((OUTER, INNER))
    starts = doc_bounds[:, 0]
    start_device = starts // block_count

    def last_open(device):
        return jnp.max(jnp.where(start_device <= device, start_device, 0))

    def next_open(device):
        count = lax.axis_size((OUTER, INNER))
        return jnp.min(jnp.where(start_device >= device, start_device, count - 1))

    block_ids = place * block_count + jnp.arange(block_count, dtype=jnp.int32)
    starts_here = jnp.any(starts[None, :] == block_ids[:, None], axis=1)
    opened = jnp.cumsum(starts_here.astype(jnp.int32))
    reach_left = opened == 0
    reach_right = opened[-1] - opened == 0

    raw_updates = jnp.einsum(
        "bthd,bthf->bhdf", key_blocks, value_blocks, preferred_element_type=jnp.float32
    )
    zero_state = jnp.zeros(raw_updates.shape[1:], jnp.float32)
    running = zero_state
    prefix_list = []
    for position in range(block_count):
        held = jnp.where(starts_here[position], zero_state, running)
        prefix_list.append(held)
        running = held + raw_updates[position]
    entering, weight_local = carried_in(
        running, last_open, False, jnp.bfloat16, jnp.bfloat16, extra=head_groups
    )
    raw_states = jnp.stack(prefix_list) + jnp.where(
        reach_left[:, None, None, None], entering[None], 0.0
    )

    qfeat = project(query_blocks, weight_local)
    kfeat = project(key_blocks, weight_local)
    weight_f = weight_local.astype(jnp.float32)
    states = jnp.einsum("hde,bhdf->bhef", weight_f, raw_states, precision=HIGH)
    state_half = states.astype(jnp.bfloat16)
    causal = jnp.arange(BLK)[:, None] >= jnp.arange(BLK)[None, :]
    scores = jnp.einsum("bthe,bshe->bhts", qfeat, kfeat, preferred_element_type=jnp.float32)
    prob_half = jnp.where(causal, scores, 0.0).astype(jnp.bfloat16)
    mixed_f = jnp.einsum("bthe,bhef->bthf", qfeat, state_half, preferred_element_type=jnp.float32)
    mixed_f = mixed_f + jnp.einsum(
        "bhts,bshf->bthf", prob_half, value_blocks, preferred_element_type=jnp.float32
    )
    gains = norm_gain.astype(jnp.float32)
    inverse = lax.rsqrt(jnp.mean(mixed_f * mixed_f, axis=-1, keepdims=True) + epsilon)
    mixed = (mixed_f * inverse * gains).astype(jnp.bfloat16)
    grad_y = out_grad.reshape(block_shape).astype(jnp.float32)
    scaled = grad_y * gains
    grad_mix = inverse * (
        scaled - mixed_f * inverse * inverse * jnp.mean(scaled * mixed_f, axis=-1, keepdims=True)
    )
    grad_half = grad_mix.astype(jnp.bfloat16)
    gain_part = jnp.sum(grad_y * mixed_f * inverse, axis=(0, 1))

    state_grads = jnp.einsum(
        "bthe,bthf->bhef", qfeat, grad_half, preferred_element_type=jnp.float32
    )
    dot_grads = jnp.einsum(
        "bthf,bshf->bhts", grad_half, value_blocks, preferred_element_type=jnp.float32
    )
    dot_half = jnp.where(causal, dot_grads, 0.0).astype(jnp.bfloat16)
    qfeat_grad = jnp.einsum(
        "bthf,bhef->bthe", grad_half, state_half, preferred_element_type=jnp.float32
    )
    qfeat_grad = (
        qfeat_grad
        + jnp.einsum("bhts,bshe->bthe", dot_half, kfeat, preferred_element_type=jnp.float32)
    ).astype(jnp.bfloat16)
    kfeat_inner = jnp.einsum(
        "bhts,bthe->bshe", dot_half, qfeat, preferred_element_type=jnp.float32
    )
    weight_part = jnp.einsum(
        "bthd,bthe->hde", query_blocks, qfeat_grad, preferred_element_type=jnp.float32
    )
    weight_part = weight_part + jnp.einsum(
        "bthd,bthe->hde", key_blocks, kfeat_inner.astype(jnp.bfloat16),
        preferred_element_type=jnp.float32,
    )
    weight_part = weight_part + jnp.einsum(
        "bhdf,bhef->hde", raw_states, state_grads, precision=HIGH
    )

    running = zero_state
    suffix_list = [zero_state] * block_count
    for position in reversed(range(block_count)):
        suffix_list[position] = running
        running = jnp.where(starts_here[position], zero_state, running + state_grads[position])
    seq_count = lax.axis_size((OUTER, INNER))
    weight_part, gain_part = summed_columns(weight_part, gain_part, last=seq_count // 2)
    leaving, (weight_part, gain_part) = carried_in(
        running, next_open, True, jnp.bfloat16, jnp.float32, tied=(weight_part, gain_part)
    )
    weight_columns, gain_sum = summed_columns(weight_part, gain_part, first=seq_count // 4)
    owned_grad = lax.all_to_all(weight_columns, "fsdp", split_axis=1, concat_axis=0, tiled=True)
    suffix = jnp.stack(suffix_list) + jnp.where(
        reach_right[:, None, None, None], leaving[None], 0.0
    )
    suffix_half = suffix.astype(jnp.bfloat16)
    kfeat_grad = jnp.einsum(
        "bshf,bhef->bshe", value_blocks, suffix_half, preferred_element_type=jnp.float32
    )
    kfeat_grad = (kfeat_grad + kfeat_inner).astype(jnp.bfloat16)
    value_grad = jnp.einsum(
        "bshe,bhef->bshf", kfeat, suffix_half, preferred_element_type=jnp.float32
    )
    value_grad = (
        value_grad
        + jnp.einsum("bhts,bthf->bshf", prob_half, grad_half, preferred_element_type=jnp.float32)
    ).astype(jnp.bfloat16)
    query_grad = jnp.einsum(
        "bthe,hde->bthd", qfeat_grad, weight_local, preferred_element_type=jnp.float32
    ).astype(jnp.bfloat16)
    key_grad = jnp.einsum(
        "bthe,hde->bthd", kfeat_grad, weight_local, preferred_element_type=jnp.float32
    ).astype(jnp.bfloat16)
    factor = (lax.axis_size((OUTER, INNER)) * tokens_here) ** (-0.5)
    flat_shape = (tokens_here, head_count * HS)
    return (
        mixed.reshape(flat_shape),
        query_grad.reshape(flat_shape),
        key_grad.reshape(flat_shape),
        value_grad.reshape(flat_shape),
        owned_grad * factor,
        gain_sum * factor,
    )


def solution(mesh):
    placed = (
        P("seq", "fsdp"),
        P("seq", "fsdp"),
        P("seq", "fsdp"),
        P(None, "fsdp", "seq"),
        P("fsdp", None),
        P(),
        P("seq", "fsdp"),
    )
    seq_count, fsdp_count = mesh.devices.shape
    inner = 8 if seq_count % 8 == 0 else seq_count
    split = jax.sharding.Mesh(
        mesh.devices.reshape(seq_count // inner, inner, fsdp_count), (OUTER, INNER, "fsdp")
    )
    seq = (OUTER, INNER)

    def respec(spec):
        return P(*[seq if part == "seq" else part for part in spec])

    placed = tuple(respec(p) for p in placed)
    return jax.shard_map(
        local,
        mesh=split,
        in_specs=placed,
        out_specs=tuple(
            respec(p)
            for p in (
                P("seq", "fsdp"),
                P("seq", "fsdp"),
                P("seq", "fsdp"),
                P("seq", "fsdp"),
                P(None, "fsdp", "seq"),
                P("fsdp", None),
            )
        ),
        check_vma=False,
    )
```

```python
import jax
import jax.numpy as jnp
from jax import lax
from jax.sharding import PartitionSpec as P

HS = 128
BLK = 128


epsilon = 1.0
HIGH = lax.Precision.HIGHEST
OUTER = "seq_row"
INNER = "seq_col"


def shifted(x, dist, backward):
    count = lax.axis_size((OUTER, INNER))
    if backward:
        pairs = [(i, i - dist) for i in range(dist, count)]
    else:
        pairs = [(i, i + dist) for i in range(count - dist)]
    return lax.ppermute(x, (OUTER, INNER), pairs)


def masked_sum(mask, stacked):
    return jnp.sum(jnp.where(mask[:, None, None, None], stacked, 0.0), 0)


def carried_in(aggregate, last_open, backward, kind, far_kind, extra=None, tied=None):
    inner = lax.axis_size(INNER)
    outer = lax.axis_size(OUTER)
    col = lax.axis_index(INNER)
    row = lax.axis_index(OUTER)
    place = row * inner + col
    near = place + 1 if backward else place - 1
    bound = last_open(near)
    cols = jnp.arange(inner)
    rows = jnp.arange(outer)
    width = aggregate.shape[-1]
    sent = aggregate.astype(kind)
    if extra is not None:
        sent = jnp.concatenate([sent, extra.astype(kind)], -1)
    in_row = lax.all_gather(sent, INNER)
    if extra is not None:
        row_extra = jnp.moveaxis(in_row[..., width:], 0, -2)
        row_extra = row_extra.reshape(row_extra.shape[:-2] + (-1,))
    in_row = in_row[..., :width].astype(jnp.float32)
    if backward:
        mine = (cols > col) & (row * inner + cols <= bound)
        row_bound = last_open(row * inner)
        carry = (row * inner + cols <= row_bound)
    else:
        mine = (cols < col) & (row * inner + cols >= bound)
        row_bound = last_open(row * inner + inner - 1)
        carry = (row * inner + cols >= row_bound)
    local_sum = masked_sum(mine, in_row)
    row_part = masked_sum(carry, in_row)
    sent = row_part.astype(far_kind)
    if tied is not None:
        sent, tied = lax.optimization_barrier((sent, tied))
    if extra is not None:
        sent = jnp.concatenate([sent, row_extra.astype(far_kind)], -1)
    across = lax.all_gather(sent, OUTER)
    if extra is not None:
        all_extra = jnp.moveaxis(across[..., width:], 0, -2)
        all_extra = all_extra.reshape(all_extra.shape[:-2] + (-1,))
    across = across[..., :width].astype(jnp.float32)
    bound_row = bound // inner
    if backward:
        take = (rows > row) & (rows <= bound_row)
    else:
        take = (rows < row) & (rows >= bound_row)
    far_sum = masked_sum(take, across)
    if extra is not None:
        return local_sum + far_sum, all_extra
    if tied is not None:
        return local_sum + far_sum, tied
    return local_sum + far_sum


def exchanged(x, bit):
    count = lax.axis_size((OUTER, INNER))
    return lax.ppermute(x, (OUTER, INNER), [(i, i ^ bit) for i in range(count)])


def gathered_columns(piece):
    count = lax.axis_size((OUTER, INNER))
    place = lax.axis_index((OUTER, INNER))
    bit = 1
    while bit < count:
        other = exchanged(piece, bit)
        upper = (place & bit) > 0
        piece = jnp.where(
            upper, jnp.concatenate([other, piece], -1), jnp.concatenate([piece, other], -1)
        )
        bit *= 2
    return piece


def summed_columns(part, extra, first=None, last=1):
    count = lax.axis_size((OUTER, INNER))
    place = lax.axis_index((OUTER, INNER))
    bit = count // 2 if first is None else first
    while bit >= last:
        half = part.shape[-1] // 2
        low, high = part[..., :half], part[..., half:]
        upper = (place & bit) > 0
        kept = jnp.where(upper, high, low)
        sent = jnp.where(upper, low, high)
        got = exchanged(jnp.concatenate([sent, extra[..., None]], -1), bit)
        part = kept + got[..., :half]
        extra = extra + got[..., half]
        bit //= 2
    return part, extra


def project(rows, weight):
    return jnp.einsum("bthd,hde->bthe", rows, weight, preferred_element_type=jnp.float32).astype(
        jnp.bfloat16
    )


def local(queries, keys, values, feature_weight, norm_gain, doc_bounds, out_grad):
    head_groups = lax.all_to_all(feature_weight, "fsdp", split_axis=0, concat_axis=1, tiled=True)
    head_count = head_groups.shape[0]
    tokens_here = queries.shape[0]
    block_count = tokens_here // BLK
    block_shape = (block_count, BLK, head_count, HS)
    query_blocks = queries.reshape(block_shape)
    key_blocks = keys.reshape(block_shape)
    value_blocks = values.reshape(block_shape)

    place = lax.axis_index((OUTER, INNER))
    starts = doc_bounds[:, 0]
    start_device = starts // block_count

    def last_open(device):
        return jnp.max(jnp.where(start_device <= device, start_device, 0))

    def next_open(device):
        count = lax.axis_size((OUTER, INNER))
        return jnp.min(jnp.where(start_device >= device, start_device, count - 1))

    block_ids = place * block_count + jnp.arange(block_count, dtype=jnp.int32)
    starts_here = jnp.any(starts[None, :] == block_ids[:, None], axis=1)
    opened = jnp.cumsum(starts_here.astype(jnp.int32))
    reach_left = opened == 0
    reach_right = opened[-1] - opened == 0

    raw_updates = jnp.einsum(
        "bthd,bthf->bhdf", key_blocks, value_blocks, preferred_element_type=jnp.float32
    )
    zero_state = jnp.zeros(raw_updates.shape[1:], jnp.float32)
    running = zero_state
    prefix_list = []
    for position in range(block_count):
        held = jnp.where(starts_here[position], zero_state, running)
        prefix_list.append(held)
        running = held + raw_updates[position]
    entering, weight_local = carried_in(
        running, last_open, False, jnp.bfloat16, jnp.bfloat16, extra=head_groups
    )
    raw_states = jnp.stack(prefix_list) + jnp.where(
        reach_left[:, None, None, None], entering[None], 0.0
    )

    qfeat = project(query_blocks, weight_local)
    kfeat = project(key_blocks, weight_local)
    weight_f = weight_local.astype(jnp.float32)
    states = jnp.einsum("hde,bhdf->bhef", weight_f, raw_states, precision=HIGH)
    state_half = states.astype(jnp.bfloat16)
    causal = jnp.arange(BLK)[:, None] >= jnp.arange(BLK)[None, :]
    scores = jnp.einsum("bthe,bshe->bhts", qfeat, kfeat, preferred_element_type=jnp.float32)
    prob_half = jnp.where(causal, scores, 0.0).astype(jnp.bfloat16)
    mixed_f = jnp.einsum("bthe,bhef->bthf", qfeat, state_half, preferred_element_type=jnp.float32)
    mixed_f = mixed_f + jnp.einsum(
        "bhts,bshf->bthf", prob_half, value_blocks, preferred_element_type=jnp.float32
    )
    gains = norm_gain.astype(jnp.float32)
    inverse = lax.rsqrt(jnp.mean(mixed_f * mixed_f, axis=-1, keepdims=True) + epsilon)
    mixed = (mixed_f * inverse * gains).astype(jnp.bfloat16)
    grad_y = out_grad.reshape(block_shape).astype(jnp.float32)
    scaled = grad_y * gains
    grad_mix = inverse * (
        scaled - mixed_f * inverse * inverse * jnp.mean(scaled * mixed_f, axis=-1, keepdims=True)
    )
    grad_half = grad_mix.astype(jnp.bfloat16)
    gain_part = jnp.sum(grad_y * mixed_f * inverse, axis=(0, 1))

    state_grads = jnp.einsum(
        "bthe,bthf->bhef", qfeat, grad_half, preferred_element_type=jnp.float32
    )
    dot_grads = jnp.einsum(
        "bthf,bshf->bhts", grad_half, value_blocks, preferred_element_type=jnp.float32
    )
    dot_half = jnp.where(causal, dot_grads, 0.0).astype(jnp.bfloat16)
    qfeat_grad = jnp.einsum(
        "bthf,bhef->bthe", grad_half, state_half, preferred_element_type=jnp.float32
    )
    qfeat_grad = (
        qfeat_grad
        + jnp.einsum("bhts,bshe->bthe", dot_half, kfeat, preferred_element_type=jnp.float32)
    ).astype(jnp.bfloat16)
    kfeat_inner = jnp.einsum(
        "bhts,bthe->bshe", dot_half, qfeat, preferred_element_type=jnp.float32
    )
    weight_part = jnp.einsum(
        "bthd,bthe->hde", query_blocks, qfeat_grad, preferred_element_type=jnp.float32
    )
    weight_part = weight_part + jnp.einsum(
        "bthd,bthe->hde", key_blocks, kfeat_inner.astype(jnp.bfloat16),
        preferred_element_type=jnp.float32,
    )
    weight_part = weight_part + jnp.einsum(
        "bhdf,bhef->hde", raw_states, state_grads, precision=HIGH
    )

    running = zero_state
    suffix_list = [zero_state] * block_count
    for position in reversed(range(block_count)):
        suffix_list[position] = running
        running = jnp.where(starts_here[position], zero_state, running + state_grads[position])
    seq_count = lax.axis_size((OUTER, INNER))
    weight_part, gain_part = summed_columns(weight_part, gain_part, last=seq_count // 4)
    leaving, (weight_part, gain_part) = carried_in(
        running, next_open, True, jnp.bfloat16, jnp.float32, tied=(weight_part, gain_part)
    )
    weight_columns, gain_sum = summed_columns(weight_part, gain_part, first=seq_count // 8)
    owned_grad = lax.all_to_all(weight_columns, "fsdp", split_axis=1, concat_axis=0, tiled=True)
    suffix = jnp.stack(suffix_list) + jnp.where(
        reach_right[:, None, None, None], leaving[None], 0.0
    )
    suffix_half = suffix.astype(jnp.bfloat16)
    kfeat_grad = jnp.einsum(
        "bshf,bhef->bshe", value_blocks, suffix_half, preferred_element_type=jnp.float32
    )
    kfeat_grad = (kfeat_grad + kfeat_inner).astype(jnp.bfloat16)
    value_grad = jnp.einsum(
        "bshe,bhef->bshf", kfeat, suffix_half, preferred_element_type=jnp.float32
    )
    value_grad = (
        value_grad
        + jnp.einsum("bhts,bthf->bshf", prob_half, grad_half, preferred_element_type=jnp.float32)
    ).astype(jnp.bfloat16)
    query_grad = jnp.einsum(
        "bthe,hde->bthd", qfeat_grad, weight_local, preferred_element_type=jnp.float32
    ).astype(jnp.bfloat16)
    key_grad = jnp.einsum(
        "bthe,hde->bthd", kfeat_grad, weight_local, preferred_element_type=jnp.float32
    ).astype(jnp.bfloat16)
    factor = (lax.axis_size((OUTER, INNER)) * tokens_here) ** (-0.5)
    flat_shape = (tokens_here, head_count * HS)
    return (
        mixed.reshape(flat_shape),
        query_grad.reshape(flat_shape),
        key_grad.reshape(flat_shape),
        value_grad.reshape(flat_shape),
        owned_grad * factor,
        gain_sum * factor,
    )


def solution(mesh):
    placed = (
        P("seq", "fsdp"),
        P("seq", "fsdp"),
        P("seq", "fsdp"),
        P(None, "fsdp", "seq"),
        P("fsdp", None),
        P(),
        P("seq", "fsdp"),
    )
    seq_count, fsdp_count = mesh.devices.shape
    inner = 8 if seq_count % 8 == 0 else seq_count
    split = jax.sharding.Mesh(
        mesh.devices.reshape(seq_count // inner, inner, fsdp_count), (OUTER, INNER, "fsdp")
    )
    seq = (OUTER, INNER)

    def respec(spec):
        return P(*[seq if part == "seq" else part for part in spec])

    placed = tuple(respec(p) for p in placed)
    return jax.shard_map(
        local,
        mesh=split,
        in_specs=placed,
        out_specs=tuple(
            respec(p)
            for p in (
                P("seq", "fsdp"),
                P("seq", "fsdp"),
                P("seq", "fsdp"),
                P("seq", "fsdp"),
                P(None, "fsdp", "seq"),
                P("fsdp", None),
            )
        ),
        check_vma=False,
    )
```
